256 devices in a mesh: req: 64 (over z, x, core), tp: 4 (over y).
Axes of the slice: x: 4, y: 4, z: 8, core: 2. Of those that a mesh axis runs over, the one named last changes fastest.
Arguments:
- layer_in: bfloat16 [8192, 2880], P('req', 'tp'), may hold values from -6 to 6
- queries: bfloat16 [8192, 4096], P('req', 'tp'), may hold values from -32 to 32
- key_values: bfloat16 [8192, 2, 512], P('req', None, 'tp'), may hold values from -12 to 12
- prefix_cache: bfloat16 [4, 1024, 2, 512], P(None, 'req', None, 'tp'), may hold values from -8 to 8
- sink_logits: float32 [64], P('tp'), may hold values from 8 to 12
- lengths: int32 [512], P('req'), may hold values from 1 to 16
- groups: int32 [512], P('req'), may hold values from 0 to 3
- batch_home: int32 [64], replicated, may hold values from 0 to 63, each once
- expert_ids: int32 [8192, 4], P('req'), may hold values from 0 to 31, all different within a row; in each aligned block of 128 rows (0 to 127, 128 to 255, ...) at most 24 rows name the same one
- router_logits: float32 [8192, 4], P('req'), may hold values from -6 to 6
- norm_gain: float32 [2880], replicated, may hold values from 0.1 to 1.9
- output_weight: bfloat16 [4096, 2880], P('tp'), may hold values from -0.09375 to 0.09375
- gate_up: bfloat16 [64, 2880, 2, 1440], P('req', None, None, 'tp'), may hold values from -0.109375 to 0.109375
- expert_down: bfloat16 [64, 1440, 2880], P('req', 'tp'), may hold values from -0.109375 to 0.109375
Outputs:
- layer_out: bfloat16 [8192, 2880], P('req', 'tp')
The draws below stay inside these ranges and needn't reach their ends.
Inputs may be any that keep to these rules, and one draw needn't show every extreme that they name: `expert_ids`: in the token slots of one index of req, no expert is named by more than 24 slots. `batch_home`: A permutation.
All inputs are finite; a program needn't handle non-finite values.
Results may differ from the reference program's by a relative error of at most 0.017.
Values may be sent and summed in bfloat16 or wider, within the bound.
No kernel may reach another device: no remote copies, remote signals or barrier semaphores. Data moves between devices by JAX's collectives and lax.ppermute only.
A program may use at most 192 MiB of HBM per device.

```python
import math
import jax
import jax.numpy as jnp
import numpy as np
from jax import lax

D = 2880
H = 64
KVH = 8
HD = 64
FF = 2880
EXPERTS = 32
TOPK = 4
PREFIX = 1024
GROUPS = 4
SUF = 16
TOK_DEV = 128
REQUESTS = 512
TOKENS = 8192
SPLIT = 2
CAP = 24
N_REQ = 64
N_TP = 4


def draw_prefix_cache(key, part):
    noise_key = jax.random.fold_in(key, 11)
    shape_all = (GROUPS, PREFIX, 2, KVH * HD)
    entries = jnp.clip(jax.random.normal(noise_key, shape_all, jnp.float32), -6.0, 6.0)
    return entries.astype(jnp.bfloat16)


def draw_queries(key, part):
    noise_key = jax.random.fold_in(key, 12)
    shape_all = (TOKENS, H * HD)
    entries = jnp.clip(3.0 * jax.random.normal(noise_key, shape_all, jnp.float32), -15.0, 15.0)
    return entries.astype(jnp.bfloat16)


def set_ends(values, stream_key, low, high):
    longest = values.shape.index(max(values.shape))
    spots = []
    for shift in (0, 1):
        where = [jax.random.randint(jax.random.fold_in(stream_key, axis), (), 0, length) for axis, length in enumerate(values.shape)]
        where[longest] = (where[longest] + shift) % values.shape[longest]
        spots.append(tuple(where))
    return values.at[spots[0]].set(low).at[spots[1]].set(high)


def steps_of(stream_key, extent, shards, least, top_value):
    def one(axis_at, blocks):
        draws = jax.random.uniform(jax.random.fold_in(jax.random.fold_in(stream_key, 6), axis_at), (blocks,), jnp.float32, least / len(shards), top_value / len(shards))
        return jnp.repeat(jnp.exp(draws), extent[axis_at] // blocks).reshape((-1,) + (1,) * (len(extent) - axis_at - 1))

    gain = one(*shards[0])
    for cut in shards[1:]:
        gain = gain * one(*cut)
    return gain


def shared_out(stream_key, own, number, rows, amount, top, bound, slope):
    order = jax.random.permutation(stream_key, amount)
    heavy_load, common = shares(amount, rows * top, bound, slope, True), shares(amount, rows * top, bound, slope, False)
    places = jnp.arange(amount)

    def named(sizes, rotation):
        used = int((sizes > 0).sum())
        fixed = max(1, used // 4)
        passed = fixed + (places - fixed + rotation * (used - fixed)) % max(1, amount - fixed)
        return jnp.zeros((amount,), jnp.int32).at[order[jnp.where(places < fixed, places, passed)]].set(jnp.asarray(sizes, jnp.int32))

    sizes = jnp.where(number % 4 == 0, named(heavy_load, number // 4), named(common, number - number // 4 - 1))
    mixed = jax.random.permutation(jax.random.fold_in(own, 3), amount)
    donor, sink = mixed[0:amount // 2 * 2:2], mixed[1:amount // 2 * 2:2]
    margin = jnp.minimum(sizes[donor] - 1, bound - sizes[sink]) // 2
    margin = jnp.where((donor == order[0]) | (sink == order[0]) | (sizes[sink] == 0), 0, jnp.maximum(margin, 0))
    passed = jax.random.randint(jax.random.fold_in(own, 4), (amount // 2,), 0, 1 << 20) % (margin + 1)
    sizes = sizes.at[donor].add(-passed).at[sink].add(passed)
    members = jnp.searchsorted(jnp.cumsum(sizes), jnp.arange(rows * top), side="right").astype(jnp.int32)
    grid = members.reshape(top, rows).T
    grid = grid[jax.random.permutation(jax.random.fold_in(own, 1), rows)]
    rotation = jax.random.randint(jax.random.fold_in(own, 2), (rows, 1), 0, top)
    return jnp.take_along_axis(grid, (jnp.arange(top)[None, :] + rotation) % top, axis=1)


def shares(amount, total, limit, lean, full):
    portions = [(1 << 20) // math.isqrt(rank ** lean) + 1 for rank in range(1, amount + 1)]
    largest = limit if full else min(limit, max(-(-total // amount), total * portions[0] // sum(portions)))
    least = 1 if total - largest >= amount - 1 else 0
    holding, surplus = [largest] + [least] * (amount - 1), total - largest - least * (amount - 1)
    while surplus > 0:
        free = [i for i in range(1, amount) if holding[i] < largest] or [i for i in range(1, amount) if holding[i] < limit]
        mass, left = sum([portions[i] for i in free]), surplus
        for i in free:
            extra = min(limit - holding[i], max(1, left * portions[i] // mass), surplus)
            holding[i] = holding[i] + extra
            surplus = surplus - extra
    return np.array(holding)


def gaussian(stream_key, extent, scale, bound, pieces=(), kind=jnp.bfloat16):
    values = jax.random.normal(stream_key, extent, jnp.float32) * scale
    if len(pieces) > 0:
        values = steps_of(stream_key, extent, pieces, -0.22, 0.18) * values
    return jnp.clip(values, min=-bound, max=bound).astype(kind)


def setup_inputs(seed: int = 0) -> dict:
    key_list = jax.random.split(jax.random.key(seed), 15)
    layer_in = gaussian(key_list[0], (TOKENS, D), 1.0, 6.0, ((0, 64), (1, 4)))
    queries = draw_queries(jax.random.fold_in(key_list[14], 71), 0)
    key_values = gaussian(key_list[2], (TOKENS, 2, KVH * HD), 2.0, 12.0, ((0, 64), (2, 4)))
    prefix_cache = draw_prefix_cache(jax.random.fold_in(key_list[14], 71), 0)
    sink_logits = jnp.clip(8.0 + 4.0 * jax.random.uniform(key_list[4], (H,), jnp.float32) ** steps_of(key_list[4], (H,), ((0, 4),), -0.2, 0.2), 8.0, 12.0)
    lengths = set_ends(jax.random.randint(key_list[5], (REQUESTS,), 1, SUF + 1), jax.random.fold_in(key_list[5], 1), 1, SUF).astype(jnp.int32)
    groups = set_ends(jax.random.randint(key_list[6], (REQUESTS,), 0, GROUPS), jax.random.fold_in(key_list[6], 1), 0, GROUPS - 1).astype(jnp.int32)
    batch_home = jax.random.permutation(key_list[7], N_REQ).astype(jnp.int32)
    expert_ids_keys = jax.random.split(jax.random.fold_in(key_list[8], 1), TOKENS // TOK_DEV)
    expert_ids_turns = jax.random.permutation(jax.random.fold_in(key_list[8], 3), TOKENS // TOK_DEV)
    expert_ids = jax.vmap(lambda own, number: shared_out(jax.random.fold_in(key_list[8], 2), own, number, TOK_DEV, EXPERTS, TOPK, CAP, 1))(expert_ids_keys, expert_ids_turns).reshape((TOKENS, TOPK))
    router_logits = gaussian(key_list[9], (TOKENS, TOPK), 1.5, 6.0, ((0, 64),), jnp.float32)
    norm_gain = jnp.clip(1.0 + 0.18 * jax.random.normal(key_list[10], (D,), jnp.float32), 0.1, 1.9)
    output_weight = gaussian(key_list[11], (H * HD, D), (H * HD) ** -0.5, 0.09375, ((0, 4),))
    gate_up = gaussian(key_list[12], (EXPERTS * SPLIT, D, 2, FF // SPLIT), D ** -0.5, 0.109375, ((0, 64), (3, 4)))
    expert_down = gaussian(key_list[13], (EXPERTS * SPLIT, FF // SPLIT, D), FF ** -0.5, 0.109375, ((0, 64), (1, 4)))
    return {"layer_in": layer_in, "queries": queries, "key_values": key_values, "prefix_cache": prefix_cache, "sink_logits": sink_logits, "lengths": lengths, "groups": groups, "batch_home": batch_home, "expert_ids": expert_ids, "router_logits": router_logits, "norm_gain": norm_gain, "output_weight": output_weight, "gate_up": gate_up, "expert_down": expert_down}


theta_base = 150000.0
norm_eps = 1e-05
logit_scale = 0.125
masked_score = -1e+30

def rotate(values, positions):
    middle = values.shape[-1] // 2
    lane_index = jnp.arange(middle, dtype=jnp.int32).astype(jnp.float32)
    inverse_freq = theta_base ** (-2.0 * lane_index / values.shape[-1])
    angles = positions.astype(jnp.float32)[:, None] * inverse_freq[None, :]
    cosine = jnp.cos(angles)[:, None, :]
    sine_part = jnp.sin(angles)[:, None, :]
    front_half = values[..., :middle]
    back_half = values[..., middle:]
    return jnp.concatenate([front_half * cosine - back_half * sine_part, back_half * cosine + front_half * sine_part], axis=-1)

def reference(layer_in, queries, key_values, prefix_cache, sink_logits, lengths, groups, batch_home, expert_ids, router_logits, norm_gain, output_weight, gate_up, expert_down):
    per_group = H // KVH
    slot_index = jnp.tile(jnp.arange(SUF, dtype=jnp.int32), REQUESTS)
    positions = PREFIX + slot_index
    rot_queries = rotate(queries.reshape(TOKENS, H, HD).astype(jnp.float32), positions).astype(jnp.bfloat16)
    rot_keys = rotate(key_values[:, 0].reshape(TOKENS, KVH, HD).astype(jnp.float32), positions).astype(jnp.bfloat16)
    fresh_values = key_values[:, 1].reshape(TOKENS, KVH, HD)
    query_groups = rot_queries.reshape(REQUESTS, SUF, KVH, per_group, HD)
    sink_values = sink_logits.reshape(KVH, per_group)

    def one_request(inputs):
        query_tile_rows, key_block, value_block, group_id, length_now = inputs
        cache_rows = lax.dynamic_index_in_dim(prefix_cache, group_id, 0, keepdims=False)
        gathered_keys = jnp.concatenate([cache_rows[:, 0].reshape(PREFIX, KVH, HD), key_block], axis=0)
        gathered_values = jnp.concatenate([cache_rows[:, 1].reshape(PREFIX, KVH, HD), value_block], axis=0)
        score_matrix = jnp.einsum('frwx,lrx->frwl', query_tile_rows.astype(jnp.float32), gathered_keys.astype(jnp.float32), precision=lax.Precision.HIGHEST) * logit_scale
        query_pos = jnp.arange(SUF, dtype=jnp.int32)[:, None]
        key_pos = jnp.arange(SUF, dtype=jnp.int32)[None, :]
        suffix_mask = (key_pos <= query_pos) & (key_pos < length_now)
        full_mask = jnp.concatenate([jnp.ones((SUF, PREFIX), dtype=bool), suffix_mask], axis=1)
        score_matrix = jnp.where(full_mask[:, None, None, :], score_matrix, masked_score)
        top_score = jnp.maximum(lax.optimization_barrier(jnp.max(score_matrix, axis=-1)), sink_values[None])
        weights = jnp.exp(score_matrix - top_score[..., None])
        totals = lax.optimization_barrier(jnp.sum(weights, axis=-1)) + jnp.exp(sink_values[None] - top_score)
        attention_probs = weights.astype(jnp.bfloat16)
        value_total = jnp.einsum('zjal,lji->zjai', attention_probs.astype(jnp.float32), gathered_values.astype(jnp.float32), precision=lax.Precision.HIGHEST)
        return (value_total / totals[..., None]).reshape(SUF, H * HD).astype(jnp.bfloat16)
    attention = lax.map(one_request, (query_groups, rot_keys.reshape(REQUESTS, SUF, KVH, HD), fresh_values.reshape(REQUESTS, SUF, KVH, HD), groups, lengths))
    attention = attention.reshape(TOKENS, H * HD)
    residual = (layer_in.astype(jnp.float32) + jnp.dot(attention, output_weight, preferred_element_type=jnp.float32)).astype(jnp.bfloat16)
    live_rows = slot_index < jnp.repeat(lengths, SUF)
    pair_weight = jnp.where(live_rows[:, None], jax.nn.softmax(router_logits, axis=-1), 0.0).astype(jnp.bfloat16)
    slot_total = N_REQ * CAP
    flat_ids = expert_ids.reshape(-1)
    onehot = (flat_ids[:, None] == jnp.arange(EXPERTS, dtype=jnp.int32)[None, :]).astype(jnp.int32)
    before = jnp.cumsum(onehot, axis=0) - onehot
    rank_in = lax.optimization_barrier(jnp.sum(before * onehot, axis=1))
    flat_slot = flat_ids * slot_total + rank_in
    pair_token = jnp.arange(TOKENS * TOPK, dtype=jnp.int32) // TOPK
    token_table = jnp.full((EXPERTS * slot_total,), TOKENS, dtype=jnp.int32).at[flat_slot].set(pair_token).reshape(EXPERTS, slot_total)
    weight_table = jnp.zeros((EXPERTS * slot_total,), jnp.bfloat16).at[flat_slot].set(pair_weight.reshape(-1)).reshape(EXPERTS, slot_total)
    split_count = max(1, N_REQ // EXPERTS)
    slab_units = FF // split_count
    part_units = slab_units // N_TP
    padded = jnp.concatenate([residual, jnp.zeros((1, D), jnp.bfloat16)], axis=0)
    first_copy = (jnp.arange(split_count, dtype=jnp.int32) == 0).astype(jnp.float32)

    def per_expert(accum, expert_index):
        token_rows = token_table[expert_index]
        row_weights = weight_table[expert_index].astype(jnp.float32)
        rows_float = padded[token_rows].astype(jnp.float32)
        row_scale = lax.rsqrt(lax.optimization_barrier(jnp.mean(rows_float * rows_float, axis=-1, keepdims=True)) + norm_eps)
        normed = (rows_float * row_scale * norm_gain[None, :]).astype(jnp.bfloat16)
        slab_in = lax.dynamic_slice_in_dim(gate_up, expert_index * split_count, split_count, 0)
        gate_and_up = jnp.einsum('nd,cdgf->ncgf', normed.astype(jnp.float32), slab_in.astype(jnp.float32), precision=lax.Precision.HIGHEST)
        hidden = (jax.nn.silu(gate_and_up[:, :, 0]) * gate_and_up[:, :, 1]).astype(jnp.bfloat16)
        slab_out = lax.dynamic_slice_in_dim(expert_down, expert_index * split_count, split_count, 0)
        hidden_parts = hidden.reshape(slot_total, split_count, N_TP, part_units).astype(jnp.float32)
        down_parts = slab_out.reshape(split_count, N_TP, part_units, D).astype(jnp.float32)
        parts = jnp.einsum('nctf,ctfd->nctd', hidden_parts, down_parts, precision=lax.Precision.HIGHEST).astype(jnp.bfloat16)
        value_total = lax.optimization_barrier(jnp.sum(parts.astype(jnp.float32), axis=2))
        result = (row_weights[:, None, None] * (value_total + first_copy[None, :, None] * rows_float[:, None, :])).astype(jnp.bfloat16)
        accum = accum.at[token_rows].add(lax.optimization_barrier(jnp.sum(result.astype(jnp.float32), axis=1)))
        return (accum, None)
    accum, _ = lax.scan(per_expert, jnp.zeros((TOKENS + 1, D), jnp.float32), jnp.arange(EXPERTS, dtype=jnp.int32))
    combined = accum[:TOKENS].astype(jnp.bfloat16)
    inverse = jnp.zeros((N_REQ,), jnp.int32).at[batch_home].set(jnp.arange(N_REQ, dtype=jnp.int32))
    return combined.reshape(N_REQ, TOK_DEV, D)[inverse].reshape(TOKENS, D)
```

```python
import jax
import jax.numpy as jnp
from jax import lax
from jax.sharding import PartitionSpec as P

D = 2880
HD = 64
EXPERTS = 32
TOPK = 4
PREFIX = 1024
CAP = 24


theta_base = 150000.0
norm_eps = 1e-05
logit_scale = 0.125
masked_score = -1e30


def rotate(values, positions):
    middle = values.shape[-1] // 2
    lane_index = jnp.arange(middle, dtype=jnp.int32).astype(jnp.float32)
    inverse_freq = theta_base ** (-2.0 * lane_index / values.shape[-1])
    angles = positions.astype(jnp.float32)[:, None] * inverse_freq[None, :]
    cosine = jnp.cos(angles)[:, None, :]
    sine_part = jnp.sin(angles)[:, None, :]
    front_half = values[..., :middle]
    back_half = values[..., middle:]
    return jnp.concatenate(
        [front_half * cosine - back_half * sine_part, back_half * cosine + front_half * sine_part],
        axis=-1,
    )


def body(
    layer_in,
    queries,
    key_values,
    prefix_cache,
    sink_logits,
    lengths,
    groups,
    batch_home,
    expert_ids,
    router_logits,
    norm_gain,
    output_weight,
    gate_up,
    expert_down,
):
    tokens = queries.shape[0]
    requests = lengths.shape[0]
    suffix = tokens // requests
    local_heads = sink_logits.shape[0]
    kv_local = key_values.shape[2] // HD
    per_group = local_heads // kv_local
    slot_index = jnp.tile(jnp.arange(suffix, dtype=jnp.int32), requests)
    positions = PREFIX + slot_index
    rotated_queries = rotate(
        queries.reshape(tokens, local_heads, HD).astype(jnp.float32), positions
    ).astype(jnp.bfloat16)
    query_groups = rotated_queries.reshape(requests, suffix, kv_local, per_group, HD)
    fresh_keys = rotate(
        key_values[:, 0].reshape(tokens, kv_local, HD).astype(jnp.float32), positions
    ).astype(jnp.bfloat16)
    fresh_keys = fresh_keys.reshape(requests, suffix, kv_local, HD)
    fresh_values = key_values[:, 1].reshape(requests, suffix, kv_local, HD)
    sink_values = sink_logits.reshape(kv_local, per_group)
    page_rows = lax.all_gather(prefix_cache, "req", axis=1, tiled=True)
    span_rows = page_rows.shape[1]
    pages_t = page_rows.reshape(page_rows.shape[0], span_rows, 2, kv_local, HD).transpose(
        0, 2, 3, 1, 4
    )
    chosen = pages_t[groups]
    prefix_keys = chosen[:, 0]
    prefix_values = chosen[:, 1]
    prefix_scores = (
        jnp.einsum(
            "rskgd,rkbd->rskgb", query_groups, prefix_keys, preferred_element_type=jnp.float32
        )
        * logit_scale
    )
    local_pos = jnp.arange(suffix, dtype=jnp.int32)
    causal = local_pos[None, :] <= local_pos[:, None]
    within = local_pos[None, None, :] < lengths[:, None, None]
    allowed = (causal[None] & within)[:, :, None, None, :]
    suffix_scores = (
        jnp.einsum(
            "rskgd,rbkd->rskgb", query_groups, fresh_keys, preferred_element_type=jnp.float32
        )
        * logit_scale
    )
    suffix_scores = jnp.where(allowed, suffix_scores, masked_score)
    top_score = jnp.maximum(
        jnp.maximum(jnp.max(prefix_scores, axis=-1), jnp.max(suffix_scores, axis=-1)),
        sink_values[None, None],
    )
    prefix_weights = jnp.exp(prefix_scores - top_score[..., None])
    suffix_weights = jnp.exp(suffix_scores - top_score[..., None])
    totals = (
        jnp.sum(prefix_weights, axis=-1)
        + jnp.sum(suffix_weights, axis=-1)
        + jnp.exp(sink_values[None, None] - top_score)
    )
    value_acc = jnp.einsum(
        "rskgb,rkbd->rskgd",
        prefix_weights.astype(jnp.bfloat16),
        prefix_values,
        preferred_element_type=jnp.float32,
    ) + jnp.einsum(
        "rskgb,rbkd->rskgd",
        suffix_weights.astype(jnp.bfloat16),
        fresh_values,
        preferred_element_type=jnp.float32,
    )
    attention = (
        (value_acc / totals[..., None]).reshape(tokens, local_heads * HD).astype(jnp.bfloat16)
    )
    partial_value = jnp.dot(attention, output_weight, preferred_element_type=jnp.float32)
    tp_index = lax.axis_index("tp")
    quarter_cols = D // lax.axis_size("tp")
    placed = lax.dynamic_update_slice_in_dim(
        jnp.zeros((tokens, D), jnp.float32),
        layer_in.astype(jnp.float32),
        tp_index * quarter_cols,
        1,
    )
    residual = lax.psum((partial_value + placed).astype(jnp.bfloat16), "tp")
    live_rows = slot_index < jnp.repeat(lengths, suffix)
    pair_weight = jnp.where(live_rows[:, None], jax.nn.softmax(router_logits, axis=-1), 0.0).astype(
        jnp.bfloat16
    )
    flat_ids = expert_ids.reshape(-1)
    onehot = (flat_ids[:, None] == jnp.arange(EXPERTS, dtype=jnp.int32)[None, :]).astype(jnp.int32)
    before = jnp.cumsum(onehot, axis=0) - onehot
    rank_in = jnp.sum(before * onehot, axis=1)
    flat_slot = flat_ids * CAP + rank_in
    pair_token = jnp.arange(tokens * TOPK, dtype=jnp.int32) // TOPK
    token_table = (
        jnp.full((EXPERTS * CAP,), tokens, dtype=jnp.int32)
        .at[flat_slot]
        .set(pair_token)
        .reshape(EXPERTS, CAP)
    )
    weight_table = (
        jnp.zeros((EXPERTS * CAP,), jnp.bfloat16)
        .at[flat_slot]
        .set(pair_weight.reshape(-1))
        .reshape(EXPERTS, CAP)
    )
    devices_req = lax.axis_size("req")
    slab_count = gate_up.shape[0]
    split_count = devices_req * slab_count // EXPERTS
    slab_ids = jnp.arange(devices_req * slab_count, dtype=jnp.int32).reshape(
        devices_req, slab_count
    )
    expert_of = slab_ids // split_count
    token_send = token_table[expert_of]
    weight_send = weight_table[expert_of]
    padded = jnp.concatenate([residual, jnp.zeros((1, residual.shape[1]), jnp.bfloat16)], axis=0)
    rows_send = padded[token_send]
    device_range = jnp.arange(devices_req, dtype=jnp.int32)
    inverse = jnp.sum(
        device_range[:, None] * (batch_home[:, None] == device_range[None, :]).astype(jnp.int32),
        axis=0,
    )
    first_copy = (
        (lax.axis_index("req") * slab_count + jnp.arange(slab_count, dtype=jnp.int32)) % split_count
        == 0
    ).astype(jnp.float32)
    rows_in = lax.all_to_all(rows_send, "req", split_axis=0, concat_axis=0, tiled=True)
    arrived_weight = lax.all_to_all(weight_send, "req", split_axis=0, concat_axis=0, tiled=True)
    arrived_token = lax.all_to_all(token_send, "req", split_axis=0, concat_axis=0, tiled=True)
    n_tp = lax.axis_size("tp")
    rows_flat = rows_in.reshape(-1, D)
    rows_float = rows_flat.astype(jnp.float32)
    row_scale = lax.rsqrt(jnp.mean(rows_float * rows_float, axis=-1, keepdims=True) + norm_eps)
    normed = (rows_float * row_scale * norm_gain).astype(jnp.bfloat16)
    gate_and_up = jnp.einsum(
        "nd,dgf->ngf", normed, gate_up[0], preferred_element_type=jnp.float32
    )
    hidden = (jax.nn.silu(gate_and_up[:, 0, :]) * gate_and_up[:, 1, :]).astype(jnp.bfloat16)
    down_chunks = expert_down[0].reshape(expert_down.shape[1], n_tp, quarter_cols)
    partial_out = jnp.einsum(
        "nf,ftd->tnd", hidden, down_chunks, preferred_element_type=jnp.float32
    )
    value_total = lax.psum_scatter(
        partial_out.astype(jnp.bfloat16), "tp", scatter_dimension=0, tiled=True
    )[0].astype(jnp.float32)
    own_rows = lax.dynamic_slice_in_dim(rows_flat, tp_index * quarter_cols, quarter_cols, 1).astype(
        jnp.float32
    )
    slab_rows = rows_in.shape[0] * rows_in.shape[2]
    result = (
        arrived_weight.reshape(slab_rows).astype(jnp.float32)[:, None]
        * (value_total + first_copy[0] * own_rows)
    ).astype(jnp.bfloat16).reshape(rows_in.shape[0], 1, rows_in.shape[2], quarter_cols)
    moved = result[inverse]
    moved_token = arrived_token[inverse]
    returned = lax.all_to_all(moved, "req", split_axis=0, concat_axis=0, tiled=True)
    returned_token = lax.all_to_all(moved_token, "req", split_axis=0, concat_axis=0, tiled=True)
    flat_rows = returned.reshape(-1, quarter_cols)
    flat_token = returned_token.reshape(-1)
    selector = (jnp.arange(tokens, dtype=jnp.int32)[:, None] == flat_token[None, :]).astype(
        jnp.bfloat16
    )
    return jnp.dot(selector, flat_rows, preferred_element_type=jnp.float32).astype(jnp.bfloat16)


def solution(mesh):
    placed = (
        P("req", "tp"),
        P("req", "tp"),
        P("req", None, "tp"),
        P(None, "req", None, "tp"),
        P("tp"),
        P("req"),
        P("req"),
        P(),
        P("req", None),
        P("req", None),
        P(),
        P("tp", None),
        P("req", None, None, "tp"),
        P("req", "tp", None),
    )
    return jax.shard_map(
        body, mesh=mesh, in_specs=placed, out_specs=P("req", "tp"), check_vma=False
    )
```

```python
import jax
import jax.numpy as jnp
from jax import lax
from jax.sharding import Mesh, PartitionSpec as P

D = 2880
HD = 64
EXPERTS = 32
TOPK = 4
PREFIX = 1024
CAP = 24


theta_base = 150000.0
norm_eps = 1e-05
logit_scale = 0.125
masked_score = -1e30


def rotate(values, positions):
    middle = values.shape[-1] // 2
    lane_index = jnp.arange(middle, dtype=jnp.int32).astype(jnp.float32)
    inverse_freq = theta_base ** (-2.0 * lane_index / values.shape[-1])
    angles = positions.astype(jnp.float32)[:, None] * inverse_freq[None, :]
    cosine = jnp.cos(angles)[:, None, :]
    sine_part = jnp.sin(angles)[:, None, :]
    front_half = values[..., :middle]
    back_half = values[..., middle:]
    return jnp.concatenate(
        [front_half * cosine - back_half * sine_part, back_half * cosine + front_half * sine_part],
        axis=-1,
    )


def body(
    layer_in,
    queries,
    key_values,
    prefix_cache,
    sink_logits,
    lengths,
    groups,
    batch_home,
    expert_ids,
    router_logits,
    norm_gain,
    output_weight,
    gate_up,
    expert_down,
):
    tokens = queries.shape[0]
    requests = lengths.shape[0]
    suffix = tokens // requests
    local_heads = sink_logits.shape[0]
    kv_local = key_values.shape[2] // HD
    per_group = local_heads // kv_local
    slot_index = jnp.tile(jnp.arange(suffix, dtype=jnp.int32), requests)
    positions = PREFIX + slot_index
    rotated_queries = rotate(
        queries.reshape(tokens, local_heads, HD).astype(jnp.float32), positions
    ).astype(jnp.bfloat16)
    query_groups = rotated_queries.reshape(requests, suffix, kv_local, per_group, HD)
    fresh_keys = rotate(
        key_values[:, 0].reshape(tokens, kv_local, HD).astype(jnp.float32), positions
    ).astype(jnp.bfloat16)
    fresh_keys = fresh_keys.reshape(requests, suffix, kv_local, HD)
    fresh_values = key_values[:, 1].reshape(requests, suffix, kv_local, HD)
    sink_values = sink_logits.reshape(kv_local, per_group)
    page_rows = lax.all_gather(prefix_cache, ("chip", "core"), axis=1, tiled=True)
    span_rows = page_rows.shape[1]
    pages_t = page_rows.reshape(page_rows.shape[0], span_rows, 2, kv_local, HD).transpose(
        0, 2, 3, 1, 4
    )
    chosen = pages_t[groups]
    prefix_keys = chosen[:, 0]
    prefix_values = chosen[:, 1]
    prefix_scores = (
        jnp.einsum(
            "rskgd,rkbd->rskgb", query_groups, prefix_keys, preferred_element_type=jnp.float32
        )
        * logit_scale
    )
    local_pos = jnp.arange(suffix, dtype=jnp.int32)
    causal = local_pos[None, :] <= local_pos[:, None]
    within = local_pos[None, None, :] < lengths[:, None, None]
    allowed = (causal[None] & within)[:, :, None, None, :]
    suffix_scores = (
        jnp.einsum(
            "rskgd,rbkd->rskgb", query_groups, fresh_keys, preferred_element_type=jnp.float32
        )
        * logit_scale
    )
    suffix_scores = jnp.where(allowed, suffix_scores, masked_score)
    top_score = jnp.maximum(
        jnp.maximum(jnp.max(prefix_scores, axis=-1), jnp.max(suffix_scores, axis=-1)),
        sink_values[None, None],
    )
    prefix_weights = jnp.exp(prefix_scores - top_score[..., None])
    suffix_weights = jnp.exp(suffix_scores - top_score[..., None])
    totals = (
        jnp.sum(prefix_weights, axis=-1)
        + jnp.sum(suffix_weights, axis=-1)
        + jnp.exp(sink_values[None, None] - top_score)
    )
    value_acc = jnp.einsum(
        "rskgb,rkbd->rskgd",
        prefix_weights.astype(jnp.bfloat16),
        prefix_values,
        preferred_element_type=jnp.float32,
    ) + jnp.einsum(
        "rskgb,rbkd->rskgd",
        suffix_weights.astype(jnp.bfloat16),
        fresh_values,
        preferred_element_type=jnp.float32,
    )
    attention = (
        (value_acc / totals[..., None]).reshape(tokens, local_heads * HD).astype(jnp.bfloat16)
    )
    n_tp = lax.axis_size("tp")
    tp_index = lax.axis_index("tp")
    core = lax.axis_index("core")
    n_chips = lax.axis_size("chip")
    quarter_cols = D // n_tp
    out_chunks = output_weight.reshape(output_weight.shape[0], n_tp, quarter_cols)
    partial_value = jnp.einsum(
        "nh,htd->tnd", attention, out_chunks, preferred_element_type=jnp.float32
    )
    own_chunk = (jnp.arange(n_tp, dtype=jnp.int32) == tp_index)[:, None, None]
    placed = jnp.where(own_chunk, layer_in.astype(jnp.float32)[None], 0.0)
    residual = lax.psum_scatter(partial_value + placed, "tp", scatter_dimension=0, tiled=True)[
        0
    ].astype(jnp.bfloat16)
    live_rows = slot_index < jnp.repeat(lengths, suffix)
    pair_weight = jnp.where(live_rows[:, None], jax.nn.softmax(router_logits, axis=-1), 0.0).astype(
        jnp.bfloat16
    )
    flat_ids = expert_ids.reshape(-1)
    onehot = (flat_ids[:, None] == jnp.arange(EXPERTS, dtype=jnp.int32)[None, :]).astype(jnp.int32)
    before = jnp.cumsum(onehot, axis=0) - onehot
    rank_in = jnp.sum(before * onehot, axis=1)
    flat_slot = flat_ids * CAP + rank_in
    pair_token = jnp.arange(tokens * TOPK, dtype=jnp.int32) // TOPK
    token_table = (
        jnp.full((EXPERTS * CAP,), tokens, dtype=jnp.int32)
        .at[flat_slot]
        .set(pair_token)
        .reshape(EXPERTS, CAP)
    )
    weight_table = (
        jnp.zeros((EXPERTS * CAP,), jnp.float32)
        .at[flat_slot]
        .set(pair_weight.reshape(-1).astype(jnp.float32))
        .reshape(EXPERTS, CAP)
    )
    meta_send = jnp.stack([token_table.astype(jnp.float32), weight_table], axis=-1)
    padded = jnp.concatenate([residual, jnp.zeros((1, quarter_cols), jnp.bfloat16)], axis=0)
    rows_send = padded[token_table]
    partner = [(0, 1), (1, 0)]
    rows_own = lax.all_to_all(rows_send, "chip", 0, 0, tiled=True)
    meta_own = lax.all_to_all(meta_send, "chip", 0, 0, tiled=True)
    rows_gathered = lax.all_gather(rows_own, "tp", axis=0, tiled=False)
    rows_other = lax.ppermute(rows_gathered, "core", partner)
    meta_other = lax.ppermute(meta_own, "core", partner)
    all_rows = jnp.concatenate([rows_gathered, rows_other], axis=1)
    all_meta = jnp.concatenate([meta_own, meta_other], axis=0)
    slab_rows = all_rows.shape[1] * all_rows.shape[2]
    rows_q = all_rows.reshape(n_tp, slab_rows, quarter_cols)
    rows_float = rows_q.astype(jnp.float32)
    row_scale = lax.rsqrt(
        jnp.mean(rows_float * rows_float, axis=(0, 2), keepdims=True) + norm_eps
    )
    gain_q = norm_gain.reshape(n_tp, 1, quarter_cols)
    normed = (rows_float * row_scale * gain_q).astype(jnp.bfloat16)
    gate_q = gate_up[0].reshape(n_tp, quarter_cols, 2, gate_up.shape[3])
    gate_and_up = jnp.einsum(
        "tnd,tdgf->ngf", normed, gate_q, preferred_element_type=jnp.float32
    )
    hidden = (jax.nn.silu(gate_and_up[:, 0, :]) * gate_and_up[:, 1, :]).astype(jnp.bfloat16)
    down_chunks = expert_down[0].reshape(expert_down.shape[1], n_tp, quarter_cols)
    partial_out = jnp.einsum(
        "nf,ftd->tnd", hidden, down_chunks, preferred_element_type=jnp.float32
    )
    value_total = lax.psum_scatter(
        partial_out.astype(jnp.bfloat16), "tp", scatter_dimension=0, tiled=True
    )[0].astype(jnp.float32)
    own_rows = lax.dynamic_index_in_dim(rows_q, tp_index, 0, keepdims=False).astype(jnp.float32)
    first_copy = (core == 0).astype(jnp.float32)
    row_weight = all_meta[..., 1].reshape(slab_rows)
    result = (row_weight[:, None] * (value_total + first_copy * own_rows)).astype(jnp.bfloat16)
    result = result.reshape(all_meta.shape[0], all_meta.shape[1], quarter_cols)
    row_token = all_meta[..., 0]
    devices_req = 2 * n_chips
    device_range = jnp.arange(devices_req, dtype=jnp.int32)
    inverse = jnp.sum(
        device_range[:, None] * (batch_home[:, None] == device_range[None, :]).astype(jnp.int32),
        axis=0,
    )
    home_chip = jnp.arange(n_chips, dtype=jnp.int32)
    keep_batch = inverse[2 * home_chip + core]
    send_batch = inverse[2 * home_chip + 1 - core]

    def local_index(batch):
        return jnp.where(batch % 2 == core, 0, n_chips) + batch // 2

    keep = result[local_index(keep_batch)]
    sent = result[local_index(send_batch)]
    received = lax.ppermute(sent, "core", partner)
    summed = (keep.astype(jnp.float32) + received.astype(jnp.float32)).astype(jnp.bfloat16)
    keep_token = row_token[local_index(keep_batch)]
    returned = lax.all_to_all(summed, "chip", 0, 0, tiled=True)
    returned_token = lax.all_to_all(keep_token, "chip", 0, 0, tiled=True)
    flat_rows = returned.reshape(-1, quarter_cols)
    flat_token = returned_token.reshape(-1).astype(jnp.int32)
    selector = (jnp.arange(tokens, dtype=jnp.int32)[:, None] == flat_token[None, :]).astype(
        jnp.bfloat16
    )
    return jnp.dot(selector, flat_rows, preferred_element_type=jnp.float32).astype(jnp.bfloat16)


def solution(mesh):
    req = ("chip", "core")
    n_req, n_tp = mesh.devices.shape
    split_mesh = Mesh(mesh.devices.reshape(n_req // 2, 2, n_tp), ("chip", "core", "tp"))
    placed = (
        P(req, "tp"),
        P(req, "tp"),
        P(req, None, "tp"),
        P(None, req, None, "tp"),
        P("tp"),
        P(req),
        P(req),
        P(),
        P(req, None),
        P(req, None),
        P(),
        P("tp", None),
        P(req, None, None, "tp"),
        P(req, "tp", None),
    )
    return jax.shard_map(
        body, mesh=split_mesh, in_specs=placed, out_specs=P(req, "tp"), check_vma=False
    )
```

```python
import jax
import jax.numpy as jnp
from jax import lax
from jax.sharding import Mesh, PartitionSpec as P

D = 2880
HD = 64
EXPERTS = 32
TOPK = 4
PREFIX = 1024
CAP = 24


theta_base = 150000.0
norm_eps = 1e-05
logit_scale = 0.125
masked_score = -1e30


def rotate(values, positions):
    middle = values.shape[-1] // 2
    lane_index = jnp.arange(middle, dtype=jnp.int32).astype(jnp.float32)
    inverse_freq = theta_base ** (-2.0 * lane_index / values.shape[-1])
    angles = positions.astype(jnp.float32)[:, None] * inverse_freq[None, :]
    cosine = jnp.cos(angles)[:, None, :]
    sine_part = jnp.sin(angles)[:, None, :]
    front_half = values[..., :middle]
    back_half = values[..., middle:]
    return jnp.concatenate(
        [front_half * cosine - back_half * sine_part, back_half * cosine + front_half * sine_part],
        axis=-1,
    )


def body(
    layer_in,
    queries,
    key_values,
    prefix_cache,
    sink_logits,
    lengths,
    groups,
    batch_home,
    expert_ids,
    router_logits,
    norm_gain,
    output_weight,
    gate_up,
    expert_down,
):
    tokens = queries.shape[0]
    requests = lengths.shape[0]
    suffix = tokens // requests
    local_heads = sink_logits.shape[0]
    kv_local = key_values.shape[2] // HD
    per_group = local_heads // kv_local
    slot_index = jnp.tile(jnp.arange(suffix, dtype=jnp.int32), requests)
    positions = PREFIX + slot_index
    rotated_queries = rotate(
        queries.reshape(tokens, local_heads, HD).astype(jnp.float32), positions
    ).astype(jnp.bfloat16)
    query_groups = rotated_queries.reshape(requests, suffix, kv_local, per_group, HD)
    fresh_keys = rotate(
        key_values[:, 0].reshape(tokens, kv_local, HD).astype(jnp.float32), positions
    ).astype(jnp.bfloat16)
    fresh_keys = fresh_keys.reshape(requests, suffix, kv_local, HD)
    fresh_values = key_values[:, 1].reshape(requests, suffix, kv_local, HD)
    sink_values = sink_logits.reshape(kv_local, per_group)
    n_chips = lax.axis_size("chip")
    partner = [(0, 1), (1, 0)]
    page_copies = jnp.broadcast_to(prefix_cache[None], (n_chips,) + prefix_cache.shape)
    pages_same_core = lax.all_to_all(page_copies, "chip", 0, 0, tiled=True)
    pages_other_core = lax.ppermute(pages_same_core, "core", partner)
    page_shards = jnp.concatenate([pages_same_core, pages_other_core], axis=0)
    shard_count, group_count, shard_rows = page_shards.shape[:3]
    span_rows = shard_count * shard_rows
    pages_t = (
        page_shards.reshape(shard_count, group_count, shard_rows, 2, kv_local, HD)
        .transpose(1, 3, 4, 0, 2, 5)
        .reshape(group_count, 2, kv_local, span_rows, HD)
    )
    chosen = pages_t[groups]
    prefix_keys = chosen[:, 0]
    prefix_values = chosen[:, 1]
    prefix_scores = (
        jnp.einsum(
            "rskgd,rkbd->rskgb", query_groups, prefix_keys, preferred_element_type=jnp.float32
        )
        * logit_scale
    )
    local_pos = jnp.arange(suffix, dtype=jnp.int32)
    causal = local_pos[None, :] <= local_pos[:, None]
    within = local_pos[None, None, :] < lengths[:, None, None]
    allowed = (causal[None] & within)[:, :, None, None, :]
    suffix_scores = (
        jnp.einsum(
            "rskgd,rbkd->rskgb", query_groups, fresh_keys, preferred_element_type=jnp.float32
        )
        * logit_scale
    )
    suffix_scores = jnp.where(allowed, suffix_scores, masked_score)
    top_score = jnp.maximum(
        jnp.maximum(jnp.max(prefix_scores, axis=-1), jnp.max(suffix_scores, axis=-1)),
        sink_values[None, None],
    )
    prefix_weights = jnp.exp(prefix_scores - top_score[..., None])
    suffix_weights = jnp.exp(suffix_scores - top_score[..., None])
    totals = (
        jnp.sum(prefix_weights, axis=-1)
        + jnp.sum(suffix_weights, axis=-1)
        + jnp.exp(sink_values[None, None] - top_score)
    )
    value_acc = jnp.einsum(
        "rskgb,rkbd->rskgd",
        prefix_weights.astype(jnp.bfloat16),
        prefix_values,
        preferred_element_type=jnp.float32,
    ) + jnp.einsum(
        "rskgb,rbkd->rskgd",
        suffix_weights.astype(jnp.bfloat16),
        fresh_values,
        preferred_element_type=jnp.float32,
    )
    attention = (
        (value_acc / totals[..., None]).reshape(tokens, local_heads * HD).astype(jnp.bfloat16)
    )
    n_tp = lax.axis_size("tp")
    tp_index = lax.axis_index("tp")
    core = lax.axis_index("core")
    chip = lax.axis_index("chip")
    quarter_cols = D // n_tp
    out_chunks = output_weight.reshape(output_weight.shape[0], n_tp, quarter_cols)
    partial_value = jnp.einsum(
        "nh,htd->tnd", attention, out_chunks, preferred_element_type=jnp.float32
    )
    own_chunk = (jnp.arange(n_tp, dtype=jnp.int32) == tp_index)[:, None, None]
    placed = jnp.where(own_chunk, layer_in.astype(jnp.float32)[None], 0.0)
    residual = lax.psum_scatter(partial_value + placed, "tp", scatter_dimension=0, tiled=True)[
        0
    ].astype(jnp.bfloat16)
    live_rows = slot_index < jnp.repeat(lengths, suffix)
    pair_weight = jnp.where(live_rows[:, None], jax.nn.softmax(router_logits, axis=-1), 0.0).astype(
        jnp.bfloat16
    )
    flat_ids = expert_ids.reshape(-1)
    onehot = (flat_ids[:, None] == jnp.arange(EXPERTS, dtype=jnp.int32)[None, :]).astype(jnp.int32)
    before = jnp.cumsum(onehot, axis=0) - onehot
    rank_in = jnp.sum(before * onehot, axis=1)
    flat_slot = flat_ids * CAP + rank_in
    pair_token = jnp.arange(tokens * TOPK, dtype=jnp.int32) // TOPK
    token_table = (
        jnp.full((EXPERTS * CAP,), tokens, dtype=jnp.int32)
        .at[flat_slot]
        .set(pair_token)
        .reshape(EXPERTS, CAP)
    )
    weight_table = (
        jnp.zeros((EXPERTS * CAP,), jnp.float32)
        .at[flat_slot]
        .set(pair_weight.reshape(-1).astype(jnp.float32))
        .reshape(EXPERTS, CAP)
    )
    meta_send = jnp.stack([token_table.astype(jnp.float32), weight_table], axis=-1)
    meta_all = lax.all_gather(meta_send, ("chip", "core"), axis=0, tiled=False)
    padded = jnp.concatenate([residual, jnp.zeros((1, quarter_cols), jnp.bfloat16)], axis=0)
    rows_send = padded[token_table]
    rows_own = lax.all_to_all(rows_send, "chip", 0, 0, tiled=True)
    rows_gathered = lax.all_gather(rows_own, "tp", axis=0, tiled=False)
    rows_other = lax.ppermute(rows_gathered, "core", partner)
    all_rows = jnp.concatenate([rows_gathered, rows_other], axis=1)
    chip_range = jnp.arange(n_chips, dtype=jnp.int32)
    source_of = jnp.concatenate([2 * chip_range + core, 2 * chip_range + 1 - core])
    all_meta = meta_all[source_of, chip]
    slab_rows = all_rows.shape[1] * all_rows.shape[2]
    rows_q = all_rows.reshape(n_tp, slab_rows, quarter_cols)
    rows_float = rows_q.astype(jnp.float32)
    row_scale = lax.rsqrt(
        jnp.mean(rows_float * rows_float, axis=(0, 2), keepdims=True) + norm_eps
    )
    gain_q = norm_gain.reshape(n_tp, 1, quarter_cols)
    normed = (
        (rows_float * row_scale * gain_q)
        .astype(jnp.bfloat16)
        .transpose(1, 0, 2)
        .reshape(slab_rows, n_tp * quarter_cols)
    )
    gate_and_up = jnp.einsum(
        "nd,dgf->ngf", normed, gate_up[0], preferred_element_type=jnp.float32
    )
    hidden = (jax.nn.silu(gate_and_up[:, 0, :]) * gate_and_up[:, 1, :]).astype(jnp.bfloat16)
    down_chunks = expert_down[0].reshape(expert_down.shape[1], n_tp, quarter_cols)
    partial_out = jnp.einsum(
        "nf,ftd->tnd", hidden, down_chunks, preferred_element_type=jnp.float32
    )
    value_total = lax.psum_scatter(
        partial_out.astype(jnp.bfloat16), "tp", scatter_dimension=0, tiled=True
    )[0].astype(jnp.float32)
    own_rows = lax.dynamic_index_in_dim(rows_q, tp_index, 0, keepdims=False).astype(jnp.float32)
    first_copy = (core == 0).astype(jnp.float32)
    row_weight = all_meta[..., 1].reshape(slab_rows)
    result = (row_weight[:, None] * (value_total + first_copy * own_rows)).astype(jnp.bfloat16)
    result = result.reshape(all_meta.shape[0], all_meta.shape[1], quarter_cols)
    devices_req = 2 * n_chips
    device_range = jnp.arange(devices_req, dtype=jnp.int32)
    inverse = jnp.sum(
        device_range[:, None] * (batch_home[:, None] == device_range[None, :]).astype(jnp.int32),
        axis=0,
    )
    keep_batch = inverse[2 * chip_range + core]
    send_batch = inverse[2 * chip_range + 1 - core]

    def local_index(batch):
        return jnp.where(batch % 2 == core, 0, n_chips) + batch // 2

    keep = result[local_index(keep_batch)]
    sent = result[local_index(send_batch)]
    received = lax.ppermute(sent, "core", partner)
    summed = (keep.astype(jnp.float32) + received.astype(jnp.float32)).astype(jnp.bfloat16)
    returned = lax.all_to_all(summed, "chip", 0, 0, tiled=True)
    home_batch = inverse[2 * chip + core]
    flat_rows = returned.reshape(-1, quarter_cols)
    flat_token = meta_all[home_batch, :, :, 0].reshape(-1).astype(jnp.int32)
    selector = (jnp.arange(tokens, dtype=jnp.int32)[:, None] == flat_token[None, :]).astype(
        jnp.bfloat16
    )
    return jnp.dot(selector, flat_rows, preferred_element_type=jnp.float32).astype(jnp.bfloat16)


def solution(mesh):
    req = ("chip", "core")
    n_req, n_tp = mesh.devices.shape
    split_mesh = Mesh(mesh.devices.reshape(n_req // 2, 2, n_tp), ("chip", "core", "tp"))
    placed = (
        P(req, "tp"),
        P(req, "tp"),
        P(req, None, "tp"),
        P(None, req, None, "tp"),
        P("tp"),
        P(req),
        P(req),
        P(),
        P(req, None),
        P(req, None),
        P(),
        P("tp", None),
        P(req, None, None, "tp"),
        P(req, "tp", None),
    )
    return jax.shard_map(
        body, mesh=split_mesh, in_specs=placed, out_specs=P(req, "tp"), check_vma=False
    )
```

```python
import jax
import jax.numpy as jnp
from jax import lax
from jax.sharding import Mesh, PartitionSpec as P

D = 2880
HD = 64
EXPERTS = 32
TOPK = 4
PREFIX = 1024
CAP = 24


theta_base = 150000.0
norm_eps = 1e-05
logit_scale = 0.125
masked_score = -1e30


def rotate(values, positions):
    middle = values.shape[-1] // 2
    lane_index = jnp.arange(middle, dtype=jnp.int32).astype(jnp.float32)
    inverse_freq = theta_base ** (-2.0 * lane_index / values.shape[-1])
    angles = positions.astype(jnp.float32)[:, None] * inverse_freq[None, :]
    cosine = jnp.cos(angles)[:, None, :]
    sine_part = jnp.sin(angles)[:, None, :]
    front_half = values[..., :middle]
    back_half = values[..., middle:]
    return jnp.concatenate(
        [front_half * cosine - back_half * sine_part, back_half * cosine + front_half * sine_part],
        axis=-1,
    )


def body(
    layer_in,
    queries,
    key_values,
    prefix_cache,
    sink_logits,
    lengths,
    groups,
    batch_home,
    expert_ids,
    router_logits,
    norm_gain,
    output_weight,
    gate_up,
    expert_down,
):
    tokens = queries.shape[0]
    requests = lengths.shape[0]
    suffix = tokens // requests
    local_heads = sink_logits.shape[0]
    kv_local = key_values.shape[2] // HD
    per_group = local_heads // kv_local
    slot_index = jnp.tile(jnp.arange(suffix, dtype=jnp.int32), requests)
    positions = PREFIX + slot_index
    rotated_queries = rotate(
        queries.reshape(tokens, local_heads, HD).astype(jnp.float32), positions
    ).astype(jnp.bfloat16)
    query_groups = rotated_queries.reshape(requests, suffix, kv_local, per_group, HD)
    fresh_keys = rotate(
        key_values[:, 0].reshape(tokens, kv_local, HD).astype(jnp.float32), positions
    ).astype(jnp.bfloat16)
    fresh_keys = fresh_keys.reshape(requests, suffix, kv_local, HD)
    fresh_values = key_values[:, 1].reshape(requests, suffix, kv_local, HD)
    sink_values = sink_logits.reshape(kv_local, per_group)
    n_chips = lax.axis_size("chip")
    core = lax.axis_index("core")
    chip = lax.axis_index("chip")
    partner = [(0, 1), (1, 0)]
    live_rows = slot_index < jnp.repeat(lengths, suffix)
    pair_weight = jnp.where(live_rows[:, None], jax.nn.softmax(router_logits, axis=-1), 0.0).astype(
        jnp.bfloat16
    )
    flat_ids = expert_ids.reshape(-1)
    onehot = (flat_ids[:, None] == jnp.arange(EXPERTS, dtype=jnp.int32)[None, :]).astype(jnp.int32)
    before = jnp.cumsum(onehot, axis=0) - onehot
    rank_in = jnp.sum(before * onehot, axis=1)
    flat_slot = flat_ids * CAP + rank_in
    pair_token = jnp.arange(tokens * TOPK, dtype=jnp.int32) // TOPK
    token_table = (
        jnp.full((EXPERTS * CAP,), tokens, dtype=jnp.int32)
        .at[flat_slot]
        .set(pair_token)
        .reshape(EXPERTS, CAP)
    )
    weight_table = (
        jnp.zeros((EXPERTS * CAP,), jnp.float32)
        .at[flat_slot]
        .set(pair_weight.reshape(-1).astype(jnp.float32))
        .reshape(EXPERTS, CAP)
    )
    meta_send = jnp.stack([token_table, weight_table], axis=-1).astype(jnp.bfloat16)
    me = 2 * chip + core
    chip_range = jnp.arange(n_chips, dtype=jnp.int32)
    home_tokens = jnp.where(
        (chip_range == batch_home[me] // 2)[:, None, None],
        token_table.astype(jnp.bfloat16)[None],
        jnp.zeros((), jnp.bfloat16),
    )
    page_width = prefix_cache.size
    meta_width = meta_send[0].size
    home_width = token_table.size
    used_width = page_width + meta_width + home_width
    bundle_width = -(-used_width // 128) * 128
    bundle = jnp.concatenate(
        [
            jnp.broadcast_to(prefix_cache.reshape(1, page_width), (n_chips, page_width)),
            meta_send.reshape(n_chips, meta_width),
            home_tokens.reshape(n_chips, home_width),
            jnp.zeros((n_chips, bundle_width - used_width), jnp.bfloat16),
        ],
        axis=1,
    )
    bundle_own = lax.all_to_all(bundle, "chip", 0, 0, tiled=True)
    bundle_other = lax.ppermute(bundle_own, "core", partner)
    bundle_all = jnp.concatenate([bundle_own, bundle_other], axis=0)
    page_shards = bundle_all[:, :page_width].reshape((2 * n_chips,) + prefix_cache.shape)
    all_meta = (
        bundle_all[:, page_width : page_width + meta_width]
        .reshape((2 * n_chips,) + meta_send.shape[1:])
        .astype(jnp.float32)
    )
    home_all = bundle_all[:, page_width + meta_width : used_width].reshape(
        (2 * n_chips,) + token_table.shape
    )
    shard_count, group_count, shard_rows = page_shards.shape[:3]
    span_rows = shard_count * shard_rows
    pages_t = (
        page_shards.reshape(shard_count, group_count, shard_rows, 2, kv_local, HD)
        .transpose(1, 3, 4, 0, 2, 5)
        .reshape(group_count, 2, kv_local, span_rows, HD)
    )
    chosen = pages_t[groups]
    prefix_keys = chosen[:, 0]
    prefix_values = chosen[:, 1]
    prefix_scores = (
        jnp.einsum(
            "rskgd,rkbd->rskgb", query_groups, prefix_keys, preferred_element_type=jnp.float32
        )
        * logit_scale
    )
    local_pos = jnp.arange(suffix, dtype=jnp.int32)
    causal = local_pos[None, :] <= local_pos[:, None]
    within = local_pos[None, None, :] < lengths[:, None, None]
    allowed = (causal[None] & within)[:, :, None, None, :]
    suffix_scores = (
        jnp.einsum(
            "rskgd,rbkd->rskgb", query_groups, fresh_keys, preferred_element_type=jnp.float32
        )
        * logit_scale
    )
    suffix_scores = jnp.where(allowed, suffix_scores, masked_score)
    top_score = jnp.maximum(
        jnp.maximum(jnp.max(prefix_scores, axis=-1), jnp.max(suffix_scores, axis=-1)),
        sink_values[None, None],
    )
    prefix_weights = jnp.exp(prefix_scores - top_score[..., None])
    suffix_weights = jnp.exp(suffix_scores - top_score[..., None])
    totals = (
        jnp.sum(prefix_weights, axis=-1)
        + jnp.sum(suffix_weights, axis=-1)
        + jnp.exp(sink_values[None, None] - top_score)
    )
    value_acc = jnp.einsum(
        "rskgb,rkbd->rskgd",
        prefix_weights.astype(jnp.bfloat16),
        prefix_values,
        preferred_element_type=jnp.float32,
    ) + jnp.einsum(
        "rskgb,rbkd->rskgd",
        suffix_weights.astype(jnp.bfloat16),
        fresh_values,
        preferred_element_type=jnp.float32,
    )
    attention = (
        (value_acc / totals[..., None]).reshape(tokens, local_heads * HD).astype(jnp.bfloat16)
    )
    n_tp = lax.axis_size("tp")
    tp_index = lax.axis_index("tp")
    quarter_cols = D // n_tp
    out_chunks = output_weight.reshape(output_weight.shape[0], n_tp, quarter_cols)
    partial_value = jnp.einsum(
        "nh,htd->tnd", attention, out_chunks, preferred_element_type=jnp.float32
    )
    own_chunk = (jnp.arange(n_tp, dtype=jnp.int32) == tp_index)[:, None, None]
    placed = jnp.where(own_chunk, layer_in.astype(jnp.float32)[None], 0.0)
    residual = lax.psum_scatter(partial_value + placed, "tp", scatter_dimension=0, tiled=True)[
        0
    ].astype(jnp.bfloat16)
    padded = jnp.concatenate([residual, jnp.zeros((1, quarter_cols), jnp.bfloat16)], axis=0)
    rows_send = padded[token_table]
    rows_own = lax.all_to_all(rows_send, "chip", 0, 0, tiled=True)
    rows_gathered = lax.all_gather(rows_own, "tp", axis=0, tiled=False)
    rows_other = lax.ppermute(rows_gathered, "core", partner)
    all_rows = jnp.concatenate([rows_gathered, rows_other], axis=1)
    slab_rows = all_rows.shape[1] * all_rows.shape[2]
    rows_q = all_rows.reshape(n_tp, slab_rows, quarter_cols)
    rows_float = rows_q.astype(jnp.float32)
    row_scale = lax.rsqrt(
        jnp.mean(rows_float * rows_float, axis=(0, 2), keepdims=True) + norm_eps
    )
    gain_q = norm_gain.reshape(n_tp, 1, quarter_cols)
    normed = (rows_float * row_scale * gain_q).astype(jnp.bfloat16)
    gate_and_up = sum(
        jnp.einsum(
            "nd,dgf->ngf",
            normed[t],
            gate_up[0, t * quarter_cols : (t + 1) * quarter_cols],
            preferred_element_type=jnp.float32,
        )
        for t in range(n_tp)
    )
    hidden = (jax.nn.silu(gate_and_up[:, 0, :]) * gate_and_up[:, 1, :]).astype(jnp.bfloat16)
    down_chunks = expert_down[0].reshape(expert_down.shape[1], n_tp, quarter_cols)
    partial_out = jnp.einsum(
        "nf,ftd->tnd", hidden, down_chunks, preferred_element_type=jnp.float32
    )
    value_total = lax.psum_scatter(
        partial_out.astype(jnp.bfloat16), "tp", scatter_dimension=0, tiled=True
    )[0].astype(jnp.float32)
    own_rows = lax.dynamic_index_in_dim(rows_q, tp_index, 0, keepdims=False).astype(jnp.float32)
    first_copy = (core == 0).astype(jnp.float32)
    row_weight = all_meta[..., 1].reshape(slab_rows)
    result = (row_weight[:, None] * (value_total + first_copy * own_rows)).astype(jnp.bfloat16)
    result = result.reshape(all_meta.shape[0], all_meta.shape[1], quarter_cols)
    devices_req = 2 * n_chips
    device_range = jnp.arange(devices_req, dtype=jnp.int32)
    inverse = jnp.sum(
        device_range[:, None] * (batch_home[:, None] == device_range[None, :]).astype(jnp.int32),
        axis=0,
    )
    keep_batch = inverse[2 * chip_range + core]
    send_batch = inverse[2 * chip_range + 1 - core]

    def local_index(batch):
        return jnp.where(batch % 2 == core, 0, n_chips) + batch // 2

    keep = result[local_index(keep_batch)]
    sent = result[local_index(send_batch)]
    received = lax.ppermute(sent, "core", partner)
    summed = (keep.astype(jnp.float32) + received.astype(jnp.float32)).astype(jnp.bfloat16)
    returned = lax.all_to_all(summed, "chip", 0, 0, tiled=True)
    home_batch = inverse[me]
    flat_rows = returned.reshape(-1, quarter_cols)
    flat_token = home_all[local_index(home_batch)].reshape(-1).astype(jnp.int32)
    selector = (jnp.arange(tokens, dtype=jnp.int32)[:, None] == flat_token[None, :]).astype(
        jnp.bfloat16
    )
    return jnp.dot(selector, flat_rows, preferred_element_type=jnp.float32).astype(jnp.bfloat16)


def solution(mesh):
    req = ("chip", "core")
    n_req, n_tp = mesh.devices.shape
    split_mesh = Mesh(mesh.devices.reshape(n_req // 2, 2, n_tp), ("chip", "core", "tp"))
    placed = (
        P(req, "tp"),
        P(req, "tp"),
        P(req, None, "tp"),
        P(None, req, None, "tp"),
        P("tp"),
        P(req),
        P(req),
        P(),
        P(req, None),
        P(req, None),
        P(),
        P("tp", None),
        P(req, None, None, "tp"),
        P(req, "tp", None),
    )
    return jax.shard_map(
        body, mesh=split_mesh, in_specs=placed, out_specs=P(req, "tp"), check_vma=False
    )
```

```python
import jax
import jax.numpy as jnp
from jax import lax
from jax.sharding import Mesh, PartitionSpec as P

D = 2880
HD = 64
EXPERTS = 32
TOPK = 4
PREFIX = 1024
CAP = 24


theta_base = 150000.0
norm_eps = 1e-05
logit_scale = 0.125
masked_score = -1e30


def rotate(values, positions):
    middle = values.shape[-1] // 2
    lane_index = jnp.arange(middle, dtype=jnp.int32).astype(jnp.float32)
    inverse_freq = theta_base ** (-2.0 * lane_index / values.shape[-1])
    angles = positions.astype(jnp.float32)[:, None] * inverse_freq[None, :]
    cosine = jnp.cos(angles)[:, None, :]
    sine_part = jnp.sin(angles)[:, None, :]
    front_half = values[..., :middle]
    back_half = values[..., middle:]
    return jnp.concatenate(
        [front_half * cosine - back_half * sine_part, back_half * cosine + front_half * sine_part],
        axis=-1,
    )


def body(
    layer_in,
    queries,
    key_values,
    prefix_cache,
    sink_logits,
    lengths,
    groups,
    batch_home,
    expert_ids,
    router_logits,
    norm_gain,
    output_weight,
    gate_up,
    expert_down,
):
    tokens = queries.shape[0]
    requests = lengths.shape[0]
    suffix = tokens // requests
    local_heads = sink_logits.shape[0]
    kv_local = key_values.shape[2] // HD
    per_group = local_heads // kv_local
    slot_index = jnp.tile(jnp.arange(suffix, dtype=jnp.int32), requests)
    positions = PREFIX + slot_index
    rotated_queries = rotate(
        queries.reshape(tokens, local_heads, HD).astype(jnp.float32), positions
    ).astype(jnp.bfloat16)
    query_groups = rotated_queries.reshape(requests, suffix, kv_local, per_group, HD)
    fresh_keys = rotate(
        key_values[:, 0].reshape(tokens, kv_local, HD).astype(jnp.float32), positions
    ).astype(jnp.bfloat16)
    fresh_keys = fresh_keys.reshape(requests, suffix, kv_local, HD)
    fresh_values = key_values[:, 1].reshape(requests, suffix, kv_local, HD)
    sink_values = sink_logits.reshape(kv_local, per_group)
    n_chips = lax.axis_size("chip")
    partner = [(0, 1), (1, 0)]
    page_copies = jnp.broadcast_to(prefix_cache[None], (n_chips,) + prefix_cache.shape)
    pages_same_core = lax.all_to_all(page_copies, "chip", 0, 0, tiled=True)
    pages_other_core = lax.ppermute(pages_same_core, "core", partner)
    page_shards = jnp.concatenate([pages_same_core, pages_other_core], axis=0)
    shard_count, group_count, shard_rows = page_shards.shape[:3]
    span_rows = shard_count * shard_rows
    pages_t = (
        page_shards.reshape(shard_count, group_count, shard_rows, 2, kv_local, HD)
        .transpose(1, 3, 4, 0, 2, 5)
        .reshape(group_count, 2, kv_local, span_rows, HD)
    )
    chosen = pages_t[groups]
    prefix_keys = chosen[:, 0]
    prefix_values = chosen[:, 1]
    prefix_scores = (
        jnp.einsum(
            "rskgd,rkbd->rskgb", query_groups, prefix_keys, preferred_element_type=jnp.float32
        )
        * logit_scale
    )
    local_pos = jnp.arange(suffix, dtype=jnp.int32)
    causal = local_pos[None, :] <= local_pos[:, None]
    within = local_pos[None, None, :] < lengths[:, None, None]
    allowed = (causal[None] & within)[:, :, None, None, :]
    suffix_scores = (
        jnp.einsum(
            "rskgd,rbkd->rskgb", query_groups, fresh_keys, preferred_element_type=jnp.float32
        )
        * logit_scale
    )
    suffix_scores = jnp.where(allowed, suffix_scores, masked_score)
    top_score = jnp.maximum(
        jnp.maximum(jnp.max(prefix_scores, axis=-1), jnp.max(suffix_scores, axis=-1)),
        sink_values[None, None],
    )
    prefix_weights = jnp.exp(prefix_scores - top_score[..., None])
    suffix_weights = jnp.exp(suffix_scores - top_score[..., None])
    totals = (
        jnp.sum(prefix_weights, axis=-1)
        + jnp.sum(suffix_weights, axis=-1)
        + jnp.exp(sink_values[None, None] - top_score)
    )
    value_acc = jnp.einsum(
        "rskgb,rkbd->rskgd",
        prefix_weights.astype(jnp.bfloat16),
        prefix_values,
        preferred_element_type=jnp.float32,
    ) + jnp.einsum(
        "rskgb,rbkd->rskgd",
        suffix_weights.astype(jnp.bfloat16),
        fresh_values,
        preferred_element_type=jnp.float32,
    )
    attention = (
        (value_acc / totals[..., None]).reshape(tokens, local_heads * HD).astype(jnp.bfloat16)
    )
    n_tp = lax.axis_size("tp")
    tp_index = lax.axis_index("tp")
    core = lax.axis_index("core")
    chip = lax.axis_index("chip")
    quarter_cols = D // n_tp
    out_chunks = output_weight.reshape(output_weight.shape[0], n_tp, quarter_cols)
    partial_value = jnp.einsum(
        "nh,htd->tnd", attention, out_chunks, preferred_element_type=jnp.float32
    )
    own_chunk = (jnp.arange(n_tp, dtype=jnp.int32) == tp_index)[:, None, None]
    placed = jnp.where(own_chunk, layer_in.astype(jnp.float32)[None], 0.0)
    residual = lax.psum_scatter(partial_value + placed, "tp", scatter_dimension=0, tiled=True)[
        0
    ].astype(jnp.bfloat16)
    live_rows = slot_index < jnp.repeat(lengths, suffix)
    pair_weight = jnp.where(live_rows[:, None], jax.nn.softmax(router_logits, axis=-1), 0.0).astype(
        jnp.bfloat16
    )
    flat_ids = expert_ids.reshape(-1)
    onehot = (flat_ids[:, None] == jnp.arange(EXPERTS, dtype=jnp.int32)[None, :]).astype(jnp.int32)
    before = jnp.cumsum(onehot, axis=0) - onehot
    rank_in = jnp.sum(before * onehot, axis=1)
    flat_slot = flat_ids * CAP + rank_in
    pair_token = jnp.arange(tokens * TOPK, dtype=jnp.int32) // TOPK
    token_table = (
        jnp.full((EXPERTS * CAP,), tokens, dtype=jnp.int32)
        .at[flat_slot]
        .set(pair_token)
        .reshape(EXPERTS, CAP)
    )
    weight_table = (
        jnp.zeros((EXPERTS * CAP,), jnp.float32)
        .at[flat_slot]
        .set(pair_weight.reshape(-1).astype(jnp.float32))
        .reshape(EXPERTS, CAP)
    )
    meta_send = jnp.stack([token_table.astype(jnp.float32), weight_table], axis=-1)
    meta_all = lax.all_gather(meta_send, ("chip", "core"), axis=0, tiled=False)
    padded = jnp.concatenate([residual, jnp.zeros((1, quarter_cols), jnp.bfloat16)], axis=0)
    rows_send = padded[token_table]
    rows_own = lax.all_to_all(rows_send, "chip", 0, 0, tiled=True)
    rows_gathered = lax.all_gather(rows_own, "tp", axis=0, tiled=False)
    rows_other = lax.ppermute(rows_gathered, "core", partner)
    all_rows = jnp.concatenate([rows_gathered, rows_other], axis=1)
    chip_range = jnp.arange(n_chips, dtype=jnp.int32)
    source_of = jnp.concatenate([2 * chip_range + core, 2 * chip_range + 1 - core])
    all_meta = meta_all[source_of, chip]
    slab_rows = all_rows.shape[1] * all_rows.shape[2]
    rows_q = all_rows.reshape(n_tp, slab_rows, quarter_cols)
    rows_float = rows_q.astype(jnp.float32)
    row_scale = lax.rsqrt(
        jnp.mean(rows_float * rows_float, axis=(0, 2), keepdims=True) + norm_eps
    )
    gain_q = norm_gain.reshape(n_tp, 1, quarter_cols)
    normed = (
        (rows_float * row_scale * gain_q)
        .astype(jnp.bfloat16)
        .transpose(1, 0, 2)
        .reshape(slab_rows, n_tp * quarter_cols)
    )
    gate_and_up = jnp.einsum(
        "nd,dgf->ngf", normed, gate_up[0], preferred_element_type=jnp.float32
    )
    hidden = (jax.nn.silu(gate_and_up[:, 0, :]) * gate_and_up[:, 1, :]).astype(jnp.bfloat16)
    half_cols = quarter_cols // 2
    down_chunks = expert_down[0].reshape(expert_down.shape[1], n_tp, 2, half_cols)
    partial_out = jnp.einsum(
        "nf,fthd->htnd", hidden, down_chunks, preferred_element_type=jnp.float32
    ).astype(jnp.bfloat16)
    half_keep = lax.dynamic_index_in_dim(partial_out, core, 0, keepdims=False)
    half_send = jnp.flip(
        lax.dynamic_index_in_dim(partial_out, 1 - core, 0, keepdims=False).reshape(
            n_tp, 2, slab_rows // 2, half_cols
        ),
        axis=1,
    ).reshape(n_tp, slab_rows, half_cols)
    half_recv = lax.ppermute(half_send, "core", partner)
    pair_sum = (half_keep.astype(jnp.float32) + half_recv.astype(jnp.float32)).astype(
        jnp.bfloat16
    )
    value_total = lax.psum_scatter(pair_sum, "tp", scatter_dimension=0, tiled=True)[0].astype(
        jnp.float32
    )
    own_rows = lax.dynamic_index_in_dim(rows_q, tp_index, 0, keepdims=False)
    own_half = lax.dynamic_index_in_dim(
        own_rows.reshape(slab_rows, 2, half_cols), core, 1, keepdims=False
    ).astype(jnp.float32)
    row_weight = all_meta[..., 1].reshape(slab_rows)
    result = (row_weight[:, None] * (value_total + own_half)).astype(jnp.bfloat16)
    result = result.reshape(all_meta.shape[0], all_meta.shape[1], half_cols)
    devices_req = 2 * n_chips
    device_range = jnp.arange(devices_req, dtype=jnp.int32)
    inverse = jnp.sum(
        device_range[:, None] * (batch_home[:, None] == device_range[None, :]).astype(jnp.int32),
        axis=0,
    )
    local_of = jnp.where(inverse % 2 == core, 0, n_chips) + inverse // 2
    sent = result[local_of]
    returned = lax.all_to_all(sent, ("chip", "core"), 0, 0, tiled=True)
    home_batch = inverse[2 * chip + core]
    flat_rows = (
        returned.reshape(n_chips, 2, all_meta.shape[1], half_cols)
        .transpose(0, 2, 1, 3)
        .reshape(-1, quarter_cols)
    )
    flat_token = meta_all[home_batch, :, :, 0].reshape(-1).astype(jnp.int32)
    selector = (jnp.arange(tokens, dtype=jnp.int32)[:, None] == flat_token[None, :]).astype(
        jnp.bfloat16
    )
    return jnp.dot(selector, flat_rows, preferred_element_type=jnp.float32).astype(jnp.bfloat16)


def solution(mesh):
    req = ("chip", "core")
    n_req, n_tp = mesh.devices.shape
    split_mesh = Mesh(mesh.devices.reshape(n_req // 2, 2, n_tp), ("chip", "core", "tp"))
    placed = (
        P(req, "tp"),
        P(req, "tp"),
        P(req, None, "tp"),
        P(None, req, None, "tp"),
        P("tp"),
        P(req),
        P(req),
        P(),
        P(req, None),
        P(req, None),
        P(),
        P("tp", None),
        P(req, None, None, "tp"),
        P(req, "tp", None),
    )
    return jax.shard_map(
        body, mesh=split_mesh, in_specs=placed, out_specs=P(req, "tp"), check_vma=False
    )
```

```python
import jax
import jax.numpy as jnp
from jax import lax
from jax.sharding import Mesh, PartitionSpec as P

D = 2880
HD = 64
EXPERTS = 32
TOPK = 4
PREFIX = 1024
CAP = 24


theta_base = 150000.0
norm_eps = 1e-05
logit_scale = 0.125
masked_score = -1e30


def rotate(values, positions):
    middle = values.shape[-1] // 2
    lane_index = jnp.arange(middle, dtype=jnp.int32).astype(jnp.float32)
    inverse_freq = theta_base ** (-2.0 * lane_index / values.shape[-1])
    angles = positions.astype(jnp.float32)[:, None] * inverse_freq[None, :]
    cosine = jnp.cos(angles)[:, None, :]
    sine_part = jnp.sin(angles)[:, None, :]
    front_half = values[..., :middle]
    back_half = values[..., middle:]
    return jnp.concatenate(
        [front_half * cosine - back_half * sine_part, back_half * cosine + front_half * sine_part],
        axis=-1,
    )


def body(
    layer_in,
    queries,
    key_values,
    prefix_cache,
    sink_logits,
    lengths,
    groups,
    batch_home,
    expert_ids,
    router_logits,
    norm_gain,
    output_weight,
    gate_up,
    expert_down,
):
    tokens = queries.shape[0]
    requests = lengths.shape[0]
    suffix = tokens // requests
    local_heads = sink_logits.shape[0]
    kv_local = key_values.shape[2] // HD
    per_group = local_heads // kv_local
    slot_index = jnp.tile(jnp.arange(suffix, dtype=jnp.int32), requests)
    positions = PREFIX + slot_index
    rotated_queries = rotate(
        queries.reshape(tokens, local_heads, HD).astype(jnp.float32), positions
    ).astype(jnp.bfloat16)
    query_groups = rotated_queries.reshape(requests, suffix, kv_local, per_group, HD)
    fresh_keys = rotate(
        key_values[:, 0].reshape(tokens, kv_local, HD).astype(jnp.float32), positions
    ).astype(jnp.bfloat16)
    fresh_keys = fresh_keys.reshape(requests, suffix, kv_local, HD)
    fresh_values = key_values[:, 1].reshape(requests, suffix, kv_local, HD)
    sink_values = sink_logits.reshape(kv_local, per_group)
    n_chips = lax.axis_size("chip")
    partner = [(0, 1), (1, 0)]
    page_copies = jnp.broadcast_to(prefix_cache[None], (n_chips,) + prefix_cache.shape)
    pages_same_core = lax.all_to_all(page_copies, "chip", 0, 0, tiled=True)
    pages_other_core = lax.ppermute(pages_same_core, "core", partner)
    page_shards = jnp.concatenate([pages_same_core, pages_other_core], axis=0)
    shard_count, group_count, shard_rows = page_shards.shape[:3]
    span_rows = shard_count * shard_rows
    pages_t = (
        page_shards.reshape(shard_count, group_count, shard_rows, 2, kv_local, HD)
        .transpose(1, 3, 4, 0, 2, 5)
        .reshape(group_count, 2, kv_local, span_rows, HD)
    )
    chosen = pages_t[groups]
    prefix_keys = chosen[:, 0]
    prefix_values = chosen[:, 1]
    prefix_scores = (
        jnp.einsum(
            "rskgd,rkbd->rskgb", query_groups, prefix_keys, preferred_element_type=jnp.float32
        )
        * logit_scale
    )
    local_pos = jnp.arange(suffix, dtype=jnp.int32)
    causal = local_pos[None, :] <= local_pos[:, None]
    within = local_pos[None, None, :] < lengths[:, None, None]
    allowed = (causal[None] & within)[:, :, None, None, :]
    suffix_scores = (
        jnp.einsum(
            "rskgd,rbkd->rskgb", query_groups, fresh_keys, preferred_element_type=jnp.float32
        )
        * logit_scale
    )
    suffix_scores = jnp.where(allowed, suffix_scores, masked_score)
    top_score = jnp.maximum(
        jnp.maximum(jnp.max(prefix_scores, axis=-1), jnp.max(suffix_scores, axis=-1)),
        sink_values[None, None],
    )
    prefix_weights = jnp.exp(prefix_scores - top_score[..., None])
    suffix_weights = jnp.exp(suffix_scores - top_score[..., None])
    totals = (
        jnp.sum(prefix_weights, axis=-1)
        + jnp.sum(suffix_weights, axis=-1)
        + jnp.exp(sink_values[None, None] - top_score)
    )
    value_acc = jnp.einsum(
        "rskgb,rkbd->rskgd",
        prefix_weights.astype(jnp.bfloat16),
        prefix_values,
        preferred_element_type=jnp.float32,
    ) + jnp.einsum(
        "rskgb,rbkd->rskgd",
        suffix_weights.astype(jnp.bfloat16),
        fresh_values,
        preferred_element_type=jnp.float32,
    )
    attention = (
        (value_acc / totals[..., None]).reshape(tokens, local_heads * HD).astype(jnp.bfloat16)
    )
    n_tp = lax.axis_size("tp")
    tp_index = lax.axis_index("tp")
    core = lax.axis_index("core")
    chip = lax.axis_index("chip")
    quarter_cols = D // n_tp
    out_chunks = output_weight.reshape(output_weight.shape[0], n_tp, quarter_cols)
    partial_value = jnp.einsum(
        "nh,htd->tnd", attention, out_chunks, preferred_element_type=jnp.float32
    )
    own_chunk = (jnp.arange(n_tp, dtype=jnp.int32) == tp_index)[:, None, None]
    placed = jnp.where(own_chunk, layer_in.astype(jnp.float32)[None], 0.0)
    residual = lax.psum_scatter(partial_value + placed, "tp", scatter_dimension=0, tiled=True)[
        0
    ].astype(jnp.bfloat16)
    live_rows = slot_index < jnp.repeat(lengths, suffix)
    pair_weight = jnp.where(live_rows[:, None], jax.nn.softmax(router_logits, axis=-1), 0.0).astype(
        jnp.bfloat16
    )
    flat_ids = expert_ids.reshape(-1)
    onehot = (flat_ids[:, None] == jnp.arange(EXPERTS, dtype=jnp.int32)[None, :]).astype(jnp.int32)
    before = jnp.cumsum(onehot, axis=0) - onehot
    rank_in = jnp.sum(before * onehot, axis=1)
    flat_slot = flat_ids * CAP + rank_in
    pair_token = jnp.arange(tokens * TOPK, dtype=jnp.int32) // TOPK
    token_table = (
        jnp.full((EXPERTS * CAP,), tokens, dtype=jnp.int32)
        .at[flat_slot]
        .set(pair_token)
        .reshape(EXPERTS, CAP)
    )
    weight_table = (
        jnp.zeros((EXPERTS * CAP,), jnp.float32)
        .at[flat_slot]
        .set(pair_weight.reshape(-1).astype(jnp.float32))
        .reshape(EXPERTS, CAP)
    )
    meta_send = jnp.stack([token_table.astype(jnp.float32), weight_table], axis=-1)
    meta_all = lax.all_gather(meta_send, ("chip", "core"), axis=0, tiled=False)
    padded = jnp.concatenate([residual, jnp.zeros((1, quarter_cols), jnp.bfloat16)], axis=0)
    rows_send = padded[token_table]
    rows_own = lax.all_to_all(rows_send, "chip", 0, 0, tiled=True)
    rows_gathered = lax.all_gather(rows_own, "tp", axis=0, tiled=False)
    meta_all, rows_gathered = lax.optimization_barrier((meta_all, rows_gathered))
    rows_other = lax.ppermute(rows_gathered, "core", partner)
    all_rows = jnp.where(
        core == 0,
        jnp.concatenate([rows_gathered, rows_other], axis=1),
        jnp.concatenate([rows_other, rows_gathered], axis=1),
    )
    chip_range = jnp.arange(n_chips, dtype=jnp.int32)
    source_of = jnp.concatenate([2 * chip_range, 2 * chip_range + 1])
    all_meta = meta_all[source_of, chip]
    slab_rows = all_rows.shape[1] * all_rows.shape[2]
    rows_q = all_rows.reshape(n_tp, slab_rows, quarter_cols)
    rows_float = rows_q.astype(jnp.float32)
    row_scale = lax.rsqrt(
        jnp.mean(rows_float * rows_float, axis=(0, 2), keepdims=True) + norm_eps
    )
    gain_q = norm_gain.reshape(n_tp, 1, quarter_cols)
    normed = (
        (rows_float * row_scale * gain_q)
        .astype(jnp.bfloat16)
        .transpose(1, 0, 2)
        .reshape(slab_rows, n_tp * quarter_cols)
    )
    gate_and_up = jnp.einsum(
        "nd,dgf->ngf", normed, gate_up[0], preferred_element_type=jnp.float32
    )
    hidden = (jax.nn.silu(gate_and_up[:, 0, :]) * gate_and_up[:, 1, :]).astype(jnp.bfloat16)
    half_cols = quarter_cols // 2
    down_chunks = expert_down[0].reshape(expert_down.shape[1], n_tp, 2, half_cols)
    partial_out = jnp.einsum(
        "nf,fthd->htnd", hidden, down_chunks, preferred_element_type=jnp.float32
    ).astype(jnp.bfloat16)
    half_keep = lax.dynamic_index_in_dim(partial_out, core, 0, keepdims=False)
    half_send = lax.dynamic_index_in_dim(partial_out, 1 - core, 0, keepdims=False)
    half_recv = lax.ppermute(half_send, "core", partner)
    pair_sum = (half_keep.astype(jnp.float32) + half_recv.astype(jnp.float32)).astype(
        jnp.bfloat16
    )
    value_total = lax.psum_scatter(pair_sum, "tp", scatter_dimension=0, tiled=True)[0].astype(
        jnp.float32
    )
    own_rows = lax.dynamic_index_in_dim(rows_q, tp_index, 0, keepdims=False)
    own_half = lax.dynamic_index_in_dim(
        own_rows.reshape(slab_rows, 2, half_cols), core, 1, keepdims=False
    ).astype(jnp.float32)
    row_weight = all_meta[..., 1].reshape(slab_rows)
    result = (row_weight[:, None] * (value_total + own_half)).astype(jnp.bfloat16)
    result = result.reshape(all_meta.shape[0], all_meta.shape[1], half_cols)
    devices_req = 2 * n_chips
    device_range = jnp.arange(devices_req, dtype=jnp.int32)
    inverse = jnp.sum(
        device_range[:, None] * (batch_home[:, None] == device_range[None, :]).astype(jnp.int32),
        axis=0,
    )
    local_of = (inverse % 2) * n_chips + inverse // 2
    sent = result[local_of]
    returned = lax.all_to_all(sent, ("chip", "core"), 0, 0, tiled=True)
    home_batch = inverse[2 * chip + core]
    flat_rows = (
        returned.reshape(n_chips, 2, all_meta.shape[1], half_cols)
        .transpose(0, 2, 1, 3)
        .reshape(-1, quarter_cols)
    )
    flat_token = meta_all[home_batch, :, :, 0].reshape(-1).astype(jnp.int32)
    selector = (jnp.arange(tokens, dtype=jnp.int32)[:, None] == flat_token[None, :]).astype(
        jnp.bfloat16
    )
    return jnp.dot(selector, flat_rows, preferred_element_type=jnp.float32).astype(jnp.bfloat16)


def solution(mesh):
    req = ("chip", "core")
    n_req, n_tp = mesh.devices.shape
    split_mesh = Mesh(mesh.devices.reshape(n_req // 2, 2, n_tp), ("chip", "core", "tp"))
    placed = (
        P(req, "tp"),
        P(req, "tp"),
        P(req, None, "tp"),
        P(None, req, None, "tp"),
        P("tp"),
        P(req),
        P(req),
        P(),
        P(req, None),
        P(req, None),
        P(),
        P("tp", None),
        P(req, None, None, "tp"),
        P(req, "tp", None),
    )
    return jax.shard_map(
        body, mesh=split_mesh, in_specs=placed, out_specs=P(req, "tp"), check_vma=False
    )
```

```python
import jax
import jax.numpy as jnp
from jax import lax
from jax.sharding import Mesh, PartitionSpec as P

D = 2880
HD = 64
EXPERTS = 32
TOPK = 4
PREFIX = 1024
CAP = 24


theta_base = 150000.0
norm_eps = 1e-05
logit_scale = 0.125
masked_score = -1e30


def rotate(values, positions):
    middle = values.shape[-1] // 2
    lane_index = jnp.arange(middle, dtype=jnp.int32).astype(jnp.float32)
    inverse_freq = theta_base ** (-2.0 * lane_index / values.shape[-1])
    angles = positions.astype(jnp.float32)[:, None] * inverse_freq[None, :]
    cosine = jnp.cos(angles)[:, None, :]
    sine_part = jnp.sin(angles)[:, None, :]
    front_half = values[..., :middle]
    back_half = values[..., middle:]
    return jnp.concatenate(
        [front_half * cosine - back_half * sine_part, back_half * cosine + front_half * sine_part],
        axis=-1,
    )


def body(
    layer_in,
    queries,
    key_values,
    prefix_cache,
    sink_logits,
    lengths,
    groups,
    batch_home,
    expert_ids,
    router_logits,
    norm_gain,
    output_weight,
    gate_up,
    expert_down,
):
    tokens = queries.shape[0]
    requests = lengths.shape[0]
    suffix = tokens // requests
    local_heads = sink_logits.shape[0]
    kv_local = key_values.shape[2] // HD
    per_group = local_heads // kv_local
    slot_index = jnp.tile(jnp.arange(suffix, dtype=jnp.int32), requests)
    positions = PREFIX + slot_index
    rotated_queries = rotate(
        queries.reshape(tokens, local_heads, HD).astype(jnp.float32), positions
    ).astype(jnp.bfloat16)
    query_groups = rotated_queries.reshape(requests, suffix, kv_local, per_group, HD)
    fresh_keys = rotate(
        key_values[:, 0].reshape(tokens, kv_local, HD).astype(jnp.float32), positions
    ).astype(jnp.bfloat16)
    fresh_keys = fresh_keys.reshape(requests, suffix, kv_local, HD)
    fresh_values = key_values[:, 1].reshape(requests, suffix, kv_local, HD)
    sink_values = sink_logits.reshape(kv_local, per_group)
    n_chips = lax.axis_size("chip")
    partner = [(0, 1), (1, 0)]
    page_copies = jnp.broadcast_to(prefix_cache[None], (n_chips,) + prefix_cache.shape)
    pages_same_core = lax.all_to_all(page_copies, "chip", 0, 0, tiled=True)
    pages_other_core = lax.ppermute(pages_same_core, "core", partner)
    page_shards = jnp.concatenate([pages_same_core, pages_other_core], axis=0)
    shard_count, group_count, shard_rows = page_shards.shape[:3]
    span_rows = shard_count * shard_rows
    pages_t = (
        page_shards.reshape(shard_count, group_count, shard_rows, 2, kv_local, HD)
        .transpose(1, 3, 4, 0, 2, 5)
        .reshape(group_count, 2, kv_local, span_rows, HD)
    )
    chosen = pages_t[groups]
    prefix_keys = chosen[:, 0]
    prefix_values = chosen[:, 1]
    prefix_scores = (
        jnp.einsum(
            "rskgd,rkbd->rskgb", query_groups, prefix_keys, preferred_element_type=jnp.float32
        )
        * logit_scale
    )
    local_pos = jnp.arange(suffix, dtype=jnp.int32)
    causal = local_pos[None, :] <= local_pos[:, None]
    within = local_pos[None, None, :] < lengths[:, None, None]
    allowed = (causal[None] & within)[:, :, None, None, :]
    suffix_scores = (
        jnp.einsum(
            "rskgd,rbkd->rskgb", query_groups, fresh_keys, preferred_element_type=jnp.float32
        )
        * logit_scale
    )
    suffix_scores = jnp.where(allowed, suffix_scores, masked_score)
    top_score = jnp.maximum(
        jnp.maximum(jnp.max(prefix_scores, axis=-1), jnp.max(suffix_scores, axis=-1)),
        sink_values[None, None],
    )
    prefix_weights = jnp.exp(prefix_scores - top_score[..., None])
    suffix_weights = jnp.exp(suffix_scores - top_score[..., None])
    totals = (
        jnp.sum(prefix_weights, axis=-1)
        + jnp.sum(suffix_weights, axis=-1)
        + jnp.exp(sink_values[None, None] - top_score)
    )
    value_acc = jnp.einsum(
        "rskgb,rkbd->rskgd",
        prefix_weights.astype(jnp.bfloat16),
        prefix_values,
        preferred_element_type=jnp.float32,
    ) + jnp.einsum(
        "rskgb,rbkd->rskgd",
        suffix_weights.astype(jnp.bfloat16),
        fresh_values,
        preferred_element_type=jnp.float32,
    )
    attention = (
        (value_acc / totals[..., None]).reshape(tokens, local_heads * HD).astype(jnp.bfloat16)
    )
    n_tp = lax.axis_size("tp")
    tp_index = lax.axis_index("tp")
    core = lax.axis_index("core")
    chip = lax.axis_index("chip")
    quarter_cols = D // n_tp
    out_chunks = output_weight.reshape(output_weight.shape[0], n_tp, quarter_cols)
    partial_value = jnp.einsum(
        "nh,htd->tnd", attention, out_chunks, preferred_element_type=jnp.float32
    )
    own_chunk = (jnp.arange(n_tp, dtype=jnp.int32) == tp_index)[:, None, None]
    placed = jnp.where(own_chunk, layer_in.astype(jnp.float32)[None], 0.0)
    residual = lax.psum_scatter(partial_value + placed, "tp", scatter_dimension=0, tiled=True)[
        0
    ].astype(jnp.bfloat16)
    live_rows = slot_index < jnp.repeat(lengths, suffix)
    pair_weight = jnp.where(live_rows[:, None], jax.nn.softmax(router_logits, axis=-1), 0.0).astype(
        jnp.bfloat16
    )
    flat_ids = expert_ids.reshape(-1)
    onehot = (flat_ids[:, None] == jnp.arange(EXPERTS, dtype=jnp.int32)[None, :]).astype(jnp.int32)
    before = jnp.cumsum(onehot, axis=0) - onehot
    rank_in = jnp.sum(before * onehot, axis=1)
    flat_slot = flat_ids * CAP + rank_in
    pair_token = jnp.arange(tokens * TOPK, dtype=jnp.int32) // TOPK
    token_table = (
        jnp.full((EXPERTS * CAP,), tokens, dtype=jnp.int32)
        .at[flat_slot]
        .set(pair_token)
        .reshape(EXPERTS, CAP)
    )
    weight_table = (
        jnp.zeros((EXPERTS * CAP,), jnp.float32)
        .at[flat_slot]
        .set(pair_weight.reshape(-1).astype(jnp.float32))
        .reshape(EXPERTS, CAP)
    )
    meta_send = jnp.stack([token_table.astype(jnp.float32), weight_table], axis=-1)
    meta_all = lax.all_gather(
        meta_send.astype(jnp.bfloat16).reshape(-1), ("chip", "core"), axis=0, tiled=False
    ).reshape((2 * n_chips,) + meta_send.shape)
    padded = jnp.concatenate([residual, jnp.zeros((1, quarter_cols), jnp.bfloat16)], axis=0)
    rows_send = padded[token_table]
    rows_own = lax.all_to_all(rows_send, "chip", 0, 0, tiled=True)
    rows_gathered = lax.all_gather(rows_own, "tp", axis=0, tiled=False)
    meta_all, rows_gathered = lax.optimization_barrier((meta_all, rows_gathered))
    rows_other = lax.ppermute(rows_gathered, "core", partner)
    all_rows = jnp.where(
        core == 0,
        jnp.concatenate([rows_gathered, rows_other], axis=1),
        jnp.concatenate([rows_other, rows_gathered], axis=1),
    )
    chip_range = jnp.arange(n_chips, dtype=jnp.int32)
    source_of = jnp.concatenate([2 * chip_range, 2 * chip_range + 1])
    all_meta = meta_all[source_of, chip]
    slab_rows = all_rows.shape[1] * all_rows.shape[2]
    rows_q = all_rows.reshape(n_tp, slab_rows, quarter_cols)
    rows_float = rows_q.astype(jnp.float32)
    row_scale = lax.rsqrt(
        jnp.mean(rows_float * rows_float, axis=(0, 2), keepdims=True) + norm_eps
    )
    gain_q = norm_gain.reshape(n_tp, 1, quarter_cols)
    normed = (rows_float * row_scale * gain_q).astype(jnp.bfloat16)
    gate_q = gate_up[0].reshape(n_tp, quarter_cols, 2, gate_up.shape[3])
    gate_and_up = jnp.einsum(
        "tnd,tdgf->ngf", normed, gate_q, preferred_element_type=jnp.float32
    )
    hidden = (jax.nn.silu(gate_and_up[:, 0, :]) * gate_and_up[:, 1, :]).astype(jnp.bfloat16)
    half_cols = quarter_cols // 2
    down_chunks = expert_down[0].reshape(expert_down.shape[1], n_tp, 2, half_cols)
    partial_out = jnp.einsum(
        "nf,fthd->htnd", hidden, down_chunks, preferred_element_type=jnp.float32
    ).astype(jnp.bfloat16)
    half_keep = lax.dynamic_index_in_dim(partial_out, core, 0, keepdims=False)
    half_send = lax.dynamic_index_in_dim(partial_out, 1 - core, 0, keepdims=False)
    half_recv = lax.ppermute(half_send, "core", partner)
    pair_sum = (half_keep.astype(jnp.float32) + half_recv.astype(jnp.float32)).astype(
        jnp.bfloat16
    )
    value_total = lax.psum_scatter(pair_sum, "tp", scatter_dimension=0, tiled=True)[0].astype(
        jnp.float32
    )
    own_rows = lax.dynamic_index_in_dim(rows_q, tp_index, 0, keepdims=False)
    own_half = lax.dynamic_index_in_dim(
        own_rows.reshape(slab_rows, 2, half_cols), core, 1, keepdims=False
    ).astype(jnp.float32)
    row_weight = all_meta[..., 1].astype(jnp.float32).reshape(slab_rows)
    result = (row_weight[:, None] * (value_total + own_half)).astype(jnp.bfloat16)
    result = result.reshape(all_meta.shape[0], all_meta.shape[1], half_cols)
    devices_req = 2 * n_chips
    device_range = jnp.arange(devices_req, dtype=jnp.int32)
    inverse = jnp.sum(
        device_range[:, None] * (batch_home[:, None] == device_range[None, :]).astype(jnp.int32),
        axis=0,
    )
    local_of = (inverse % 2) * n_chips + inverse // 2
    sent = result[local_of]
    returned = lax.all_to_all(sent, ("chip", "core"), 0, 0, tiled=True)
    home_batch = inverse[2 * chip + core]
    flat_rows = (
        returned.reshape(n_chips, 2, all_meta.shape[1], half_cols)
        .transpose(0, 2, 1, 3)
        .reshape(-1, quarter_cols)
    )
    flat_token = meta_all[home_batch, :, :, 0].reshape(-1).astype(jnp.int32)
    selector = (jnp.arange(tokens, dtype=jnp.int32)[:, None] == flat_token[None, :]).astype(
        jnp.bfloat16
    )
    return jnp.dot(selector, flat_rows, preferred_element_type=jnp.float32).astype(jnp.bfloat16)


def solution(mesh):
    req = ("chip", "core")
    n_req, n_tp = mesh.devices.shape
    split_mesh = Mesh(mesh.devices.reshape(n_req // 2, 2, n_tp), ("chip", "core", "tp"))
    placed = (
        P(req, "tp"),
        P(req, "tp"),
        P(req, None, "tp"),
        P(None, req, None, "tp"),
        P("tp"),
        P(req),
        P(req),
        P(),
        P(req, None),
        P(req, None),
        P(),
        P("tp", None),
        P(req, None, None, "tp"),
        P(req, "tp", None),
    )
    return jax.shard_map(
        body, mesh=split_mesh, in_specs=placed, out_specs=P(req, "tp"), check_vma=False
    )
```

```python
import jax
import jax.numpy as jnp
from jax import lax
from jax.sharding import Mesh, PartitionSpec as P

D = 2880
HD = 64
EXPERTS = 32
TOPK = 4
PREFIX = 1024
CAP = 24


theta_base = 150000.0
norm_eps = 1e-05
logit_scale = 0.125
masked_score = -1e30


def rotate(values, positions):
    middle = values.shape[-1] // 2
    lane_index = jnp.arange(middle, dtype=jnp.int32).astype(jnp.float32)
    inverse_freq = theta_base ** (-2.0 * lane_index / values.shape[-1])
    angles = positions.astype(jnp.float32)[:, None] * inverse_freq[None, :]
    cosine = jnp.cos(angles)[:, None, :]
    sine_part = jnp.sin(angles)[:, None, :]
    front_half = values[..., :middle]
    back_half = values[..., middle:]
    return jnp.concatenate(
        [front_half * cosine - back_half * sine_part, back_half * cosine + front_half * sine_part],
        axis=-1,
    )


def body(
    layer_in,
    queries,
    key_values,
    prefix_cache,
    sink_logits,
    lengths,
    groups,
    batch_home,
    expert_ids,
    router_logits,
    norm_gain,
    output_weight,
    gate_up,
    expert_down,
):
    tokens = queries.shape[0]
    requests = lengths.shape[0]
    suffix = tokens // requests
    local_heads = sink_logits.shape[0]
    kv_local = key_values.shape[2] // HD
    per_group = local_heads // kv_local
    slot_index = jnp.tile(jnp.arange(suffix, dtype=jnp.int32), requests)
    positions = PREFIX + slot_index
    rotated_queries = rotate(
        queries.reshape(tokens, local_heads, HD).astype(jnp.float32), positions
    ).astype(jnp.bfloat16)
    query_groups = rotated_queries.reshape(requests, suffix, kv_local, per_group, HD)
    fresh_keys = rotate(
        key_values[:, 0].reshape(tokens, kv_local, HD).astype(jnp.float32), positions
    ).astype(jnp.bfloat16)
    fresh_keys = fresh_keys.reshape(requests, suffix, kv_local, HD)
    fresh_values = key_values[:, 1].reshape(requests, suffix, kv_local, HD)
    sink_values = sink_logits.reshape(kv_local, per_group)
    n_chips = lax.axis_size("chip")
    partner = [(0, 1), (1, 0)]
    page_copies = jnp.broadcast_to(prefix_cache[None], (n_chips,) + prefix_cache.shape)
    pages_same_core = lax.all_to_all(page_copies, "chip", 0, 0, tiled=True)
    pages_other_core = lax.ppermute(pages_same_core, "core", partner)
    page_shards = jnp.concatenate([pages_same_core, pages_other_core], axis=0)
    shard_count, group_count, shard_rows = page_shards.shape[:3]
    span_rows = shard_count * shard_rows
    pages_t = (
        page_shards.reshape(shard_count, group_count, shard_rows, 2, kv_local, HD)
        .transpose(1, 3, 4, 0, 2, 5)
        .reshape(group_count, 2, kv_local, span_rows, HD)
    )
    chosen = pages_t[groups]
    prefix_keys = chosen[:, 0]
    prefix_values = chosen[:, 1]
    prefix_scores = (
        jnp.einsum(
            "rskgd,rkbd->rskgb", query_groups, prefix_keys, preferred_element_type=jnp.float32
        )
        * logit_scale
    )
    local_pos = jnp.arange(suffix, dtype=jnp.int32)
    causal = local_pos[None, :] <= local_pos[:, None]
    within = local_pos[None, None, :] < lengths[:, None, None]
    allowed = (causal[None] & within)[:, :, None, None, :]
    suffix_scores = (
        jnp.einsum(
            "rskgd,rbkd->rskgb", query_groups, fresh_keys, preferred_element_type=jnp.float32
        )
        * logit_scale
    )
    suffix_scores = jnp.where(allowed, suffix_scores, masked_score)
    top_score = jnp.maximum(
        jnp.maximum(jnp.max(prefix_scores, axis=-1), jnp.max(suffix_scores, axis=-1)),
        sink_values[None, None],
    )
    prefix_weights = jnp.exp(prefix_scores - top_score[..., None])
    suffix_weights = jnp.exp(suffix_scores - top_score[..., None])
    totals = (
        jnp.sum(prefix_weights, axis=-1)
        + jnp.sum(suffix_weights, axis=-1)
        + jnp.exp(sink_values[None, None] - top_score)
    )
    value_acc = jnp.einsum(
        "rskgb,rkbd->rskgd",
        prefix_weights.astype(jnp.bfloat16),
        prefix_values,
        preferred_element_type=jnp.float32,
    ) + jnp.einsum(
        "rskgb,rbkd->rskgd",
        suffix_weights.astype(jnp.bfloat16),
        fresh_values,
        preferred_element_type=jnp.float32,
    )
    attention = (
        (value_acc / totals[..., None]).reshape(tokens, local_heads * HD).astype(jnp.bfloat16)
    )
    n_tp = lax.axis_size("tp")
    tp_index = lax.axis_index("tp")
    core = lax.axis_index("core")
    chip = lax.axis_index("chip")
    quarter_cols = D // n_tp
    out_chunks = output_weight.reshape(output_weight.shape[0], n_tp, quarter_cols)
    partial_value = jnp.einsum(
        "nh,htd->tnd", attention, out_chunks, preferred_element_type=jnp.float32
    )
    own_chunk = (jnp.arange(n_tp, dtype=jnp.int32) == tp_index)[:, None, None]
    placed = jnp.where(own_chunk, layer_in.astype(jnp.float32)[None], 0.0)
    residual = lax.psum_scatter(
        (partial_value + placed).astype(jnp.bfloat16), "tp", scatter_dimension=0, tiled=True
    )[0]
    live_rows = slot_index < jnp.repeat(lengths, suffix)
    pair_weight = jnp.where(live_rows[:, None], jax.nn.softmax(router_logits, axis=-1), 0.0).astype(
        jnp.bfloat16
    )
    flat_ids = expert_ids.reshape(-1)
    onehot = (flat_ids[:, None] == jnp.arange(EXPERTS, dtype=jnp.int32)[None, :]).astype(jnp.int32)
    before = jnp.cumsum(onehot, axis=0) - onehot
    rank_in = jnp.sum(before * onehot, axis=1)
    flat_slot = flat_ids * CAP + rank_in
    pair_token = jnp.arange(tokens * TOPK, dtype=jnp.int32) // TOPK
    token_table = (
        jnp.full((EXPERTS * CAP,), tokens, dtype=jnp.int32)
        .at[flat_slot]
        .set(pair_token)
        .reshape(EXPERTS, CAP)
    )
    weight_table = (
        jnp.zeros((EXPERTS * CAP,), jnp.float32)
        .at[flat_slot]
        .set(pair_weight.reshape(-1).astype(jnp.float32))
        .reshape(EXPERTS, CAP)
    )
    meta_send = jnp.stack([token_table.astype(jnp.float32), weight_table], axis=-1)
    meta_all = lax.all_gather(
        meta_send.astype(jnp.bfloat16).reshape(-1), ("chip", "core"), axis=0, tiled=False
    ).reshape((2 * n_chips,) + meta_send.shape)
    padded = jnp.concatenate([residual, jnp.zeros((1, quarter_cols), jnp.bfloat16)], axis=0)
    rows_send = padded[token_table]
    rows_own = lax.all_to_all(rows_send, "chip", 0, 0, tiled=True)
    rows_gathered = lax.all_gather(rows_own, "tp", axis=0, tiled=False)
    meta_all, rows_gathered = lax.optimization_barrier((meta_all, rows_gathered))
    rows_other = lax.ppermute(rows_gathered, "core", partner)
    all_rows = jnp.where(
        core == 0,
        jnp.concatenate([rows_gathered, rows_other], axis=1),
        jnp.concatenate([rows_other, rows_gathered], axis=1),
    )
    chip_range = jnp.arange(n_chips, dtype=jnp.int32)
    source_of = jnp.concatenate([2 * chip_range, 2 * chip_range + 1])
    all_meta = meta_all[source_of, chip]
    slab_rows = all_rows.shape[1] * all_rows.shape[2]
    rows_q = all_rows.reshape(n_tp, slab_rows, quarter_cols)
    rows_float = rows_q.astype(jnp.float32)
    row_scale = lax.rsqrt(
        jnp.mean(rows_float * rows_float, axis=(0, 2), keepdims=True) + norm_eps
    )
    gain_q = norm_gain.reshape(n_tp, 1, quarter_cols)
    normed = (rows_float * row_scale * gain_q).astype(jnp.bfloat16)
    gate_q = gate_up[0].reshape(n_tp, quarter_cols, 2, gate_up.shape[3])
    gate_and_up = jnp.einsum(
        "tnd,tdgf->ngf", normed, gate_q, preferred_element_type=jnp.float32
    )
    hidden = (jax.nn.silu(gate_and_up[:, 0, :]) * gate_and_up[:, 1, :]).astype(jnp.bfloat16)
    half_cols = quarter_cols // 2
    down_chunks = expert_down[0].reshape(expert_down.shape[1], n_tp, 2, half_cols)
    partial_out = jnp.einsum(
        "nf,fthd->htnd", hidden, down_chunks, preferred_element_type=jnp.float32
    ).astype(jnp.bfloat16)
    half_keep = lax.dynamic_index_in_dim(partial_out, core, 0, keepdims=False)
    half_send = lax.dynamic_index_in_dim(partial_out, 1 - core, 0, keepdims=False)
    half_recv = lax.ppermute(half_send, "core", partner)
    pair_sum = (half_keep.astype(jnp.float32) + half_recv.astype(jnp.float32)).astype(
        jnp.bfloat16
    )
    value_total = lax.psum_scatter(pair_sum, "tp", scatter_dimension=0, tiled=True)[0].astype(
        jnp.float32
    )
    own_rows = lax.dynamic_index_in_dim(rows_q, tp_index, 0, keepdims=False)
    own_half = lax.dynamic_index_in_dim(
        own_rows.reshape(slab_rows, 2, half_cols), core, 1, keepdims=False
    ).astype(jnp.float32)
    row_weight = all_meta[..., 1].astype(jnp.float32).reshape(slab_rows)
    result = (row_weight[:, None] * (value_total + own_half)).astype(jnp.bfloat16)
    result = result.reshape(all_meta.shape[0], all_meta.shape[1], half_cols)
    devices_req = 2 * n_chips
    device_range = jnp.arange(devices_req, dtype=jnp.int32)
    inverse = jnp.sum(
        device_range[:, None] * (batch_home[:, None] == device_range[None, :]).astype(jnp.int32),
        axis=0,
    )
    local_of = (inverse % 2) * n_chips + inverse // 2
    sent = result[local_of]
    returned = lax.all_to_all(sent, ("chip", "core"), 0, 0, tiled=True)
    home_batch = inverse[2 * chip + core]
    flat_rows = (
        returned.reshape(n_chips, 2, all_meta.shape[1], half_cols)
        .transpose(0, 2, 1, 3)
        .reshape(-1, quarter_cols)
    )
    flat_token = meta_all[home_batch, :, :, 0].reshape(-1).astype(jnp.int32)
    selector = (jnp.arange(tokens, dtype=jnp.int32)[:, None] == flat_token[None, :]).astype(
        jnp.bfloat16
    )
    return jnp.dot(selector, flat_rows, preferred_element_type=jnp.float32).astype(jnp.bfloat16)


def solution(mesh):
    req = ("chip", "core")
    n_req, n_tp = mesh.devices.shape
    split_mesh = Mesh(mesh.devices.reshape(n_req // 2, 2, n_tp), ("chip", "core", "tp"))
    placed = (
        P(req, "tp"),
        P(req, "tp"),
        P(req, None, "tp"),
        P(None, req, None, "tp"),
        P("tp"),
        P(req),
        P(req),
        P(),
        P(req, None),
        P(req, None),
        P(),
        P("tp", None),
        P(req, None, None, "tp"),
        P(req, "tp", None),
    )
    return jax.shard_map(
        body, mesh=split_mesh, in_specs=placed, out_specs=P(req, "tp"), check_vma=False
    )
```

```python
import jax
import jax.numpy as jnp
from jax import lax
from jax.sharding import Mesh, PartitionSpec as P

D = 2880
HD = 64
EXPERTS = 32
TOPK = 4
PREFIX = 1024
CAP = 24


theta_base = 150000.0
norm_eps = 1e-05
logit_scale = 0.125
masked_score = -1e30


def rotate(values, positions):
    middle = values.shape[-1] // 2
    lane_index = jnp.arange(middle, dtype=jnp.int32).astype(jnp.float32)
    inverse_freq = theta_base ** (-2.0 * lane_index / values.shape[-1])
    angles = positions.astype(jnp.float32)[:, None] * inverse_freq[None, :]
    cosine = jnp.cos(angles)[:, None, :]
    sine_part = jnp.sin(angles)[:, None, :]
    front_half = values[..., :middle]
    back_half = values[..., middle:]
    return jnp.concatenate(
        [front_half * cosine - back_half * sine_part, back_half * cosine + front_half * sine_part],
        axis=-1,
    )


def body(
    layer_in,
    queries,
    key_values,
    prefix_cache,
    sink_logits,
    lengths,
    groups,
    batch_home,
    expert_ids,
    router_logits,
    norm_gain,
    output_weight,
    gate_up,
    expert_down,
):
    tokens = queries.shape[0]
    requests = lengths.shape[0]
    suffix = tokens // requests
    local_heads = sink_logits.shape[0]
    kv_local = key_values.shape[2] // HD
    per_group = local_heads // kv_local
    slot_index = jnp.tile(jnp.arange(suffix, dtype=jnp.int32), requests)
    positions = PREFIX + slot_index
    rotated_queries = rotate(
        queries.reshape(tokens, local_heads, HD).astype(jnp.float32), positions
    ).astype(jnp.bfloat16)
    query_groups = rotated_queries.reshape(requests, suffix, kv_local, per_group, HD)
    fresh_keys = rotate(
        key_values[:, 0].reshape(tokens, kv_local, HD).astype(jnp.float32), positions
    ).astype(jnp.bfloat16)
    fresh_keys = fresh_keys.reshape(requests, suffix, kv_local, HD)
    fresh_values = key_values[:, 1].reshape(requests, suffix, kv_local, HD)
    sink_values = sink_logits.reshape(kv_local, per_group)
    n_chips = lax.axis_size("chip")
    partner = [(0, 1), (1, 0)]
    page_copies = jnp.broadcast_to(prefix_cache[None], (n_chips,) + prefix_cache.shape)
    pages_same_core = lax.all_to_all(page_copies, "chip", 0, 0, tiled=True)
    pages_other_core = lax.ppermute(pages_same_core, "core", partner)
    page_shards = jnp.concatenate([pages_same_core, pages_other_core], axis=0)
    shard_count, group_count, shard_rows = page_shards.shape[:3]
    span_rows = shard_count * shard_rows
    pages_t = (
        page_shards.reshape(shard_count, group_count, shard_rows, 2, kv_local, HD)
        .transpose(1, 3, 4, 0, 2, 5)
        .reshape(group_count, 2, kv_local, span_rows, HD)
    )
    chosen = pages_t[groups]
    prefix_keys = chosen[:, 0]
    prefix_values = chosen[:, 1]
    prefix_scores = (
        jnp.einsum(
            "rskgd,rkbd->rskgb", query_groups, prefix_keys, preferred_element_type=jnp.float32
        )
        * logit_scale
    )
    local_pos = jnp.arange(suffix, dtype=jnp.int32)
    causal = local_pos[None, :] <= local_pos[:, None]
    within = local_pos[None, None, :] < lengths[:, None, None]
    allowed = (causal[None] & within)[:, :, None, None, :]
    suffix_scores = (
        jnp.einsum(
            "rskgd,rbkd->rskgb", query_groups, fresh_keys, preferred_element_type=jnp.float32
        )
        * logit_scale
    )
    suffix_scores = jnp.where(allowed, suffix_scores, masked_score)
    top_score = jnp.maximum(
        jnp.maximum(jnp.max(prefix_scores, axis=-1), jnp.max(suffix_scores, axis=-1)),
        sink_values[None, None],
    )
    prefix_weights = jnp.exp(prefix_scores - top_score[..., None])
    suffix_weights = jnp.exp(suffix_scores - top_score[..., None])
    totals = (
        jnp.sum(prefix_weights, axis=-1)
        + jnp.sum(suffix_weights, axis=-1)
        + jnp.exp(sink_values[None, None] - top_score)
    )
    value_acc = jnp.einsum(
        "rskgb,rkbd->rskgd",
        prefix_weights.astype(jnp.bfloat16),
        prefix_values,
        preferred_element_type=jnp.float32,
    ) + jnp.einsum(
        "rskgb,rbkd->rskgd",
        suffix_weights.astype(jnp.bfloat16),
        fresh_values,
        preferred_element_type=jnp.float32,
    )
    attention = (
        (value_acc / totals[..., None]).reshape(tokens, local_heads * HD).astype(jnp.bfloat16)
    )
    n_tp = lax.axis_size("tp")
    tp_index = lax.axis_index("tp")
    core = lax.axis_index("core")
    chip = lax.axis_index("chip")
    quarter_cols = D // n_tp
    out_chunks = output_weight.reshape(output_weight.shape[0], n_tp, quarter_cols)
    partial_value = jnp.einsum(
        "nh,htd->tnd", attention, out_chunks, preferred_element_type=jnp.float32
    )
    own_chunk = (jnp.arange(n_tp, dtype=jnp.int32) == tp_index)[:, None, None]
    placed = jnp.where(own_chunk, layer_in.astype(jnp.float32)[None], 0.0)
    residual = lax.psum_scatter(
        (partial_value + placed).astype(jnp.bfloat16), "tp", scatter_dimension=0, tiled=True
    )[0]
    live_rows = slot_index < jnp.repeat(lengths, suffix)
    pair_weight = jnp.where(live_rows[:, None], jax.nn.softmax(router_logits, axis=-1), 0.0).astype(
        jnp.bfloat16
    )
    flat_ids = expert_ids.reshape(-1)
    onehot = (flat_ids[:, None] == jnp.arange(EXPERTS, dtype=jnp.int32)[None, :]).astype(jnp.int32)
    before = jnp.cumsum(onehot, axis=0) - onehot
    rank_in = jnp.sum(before * onehot, axis=1)
    flat_slot = flat_ids * CAP + rank_in
    pair_token = jnp.arange(tokens * TOPK, dtype=jnp.int32) // TOPK
    token_table = (
        jnp.full((EXPERTS * CAP,), tokens, dtype=jnp.int32)
        .at[flat_slot]
        .set(pair_token)
        .reshape(EXPERTS, CAP)
    )
    weight_table = (
        jnp.zeros((EXPERTS * CAP,), jnp.float32)
        .at[flat_slot]
        .set(pair_weight.reshape(-1).astype(jnp.float32))
        .reshape(EXPERTS, CAP)
    )
    meta_send = jnp.stack([token_table.astype(jnp.float32), weight_table], axis=-1)
    meta_all = lax.all_gather(
        meta_send.astype(jnp.bfloat16).reshape(-1), ("chip", "core"), axis=0, tiled=False
    ).reshape((2 * n_chips,) + meta_send.shape)
    padded = jnp.concatenate([residual, jnp.zeros((1, quarter_cols), jnp.bfloat16)], axis=0)
    rows_send = padded[token_table]
    cut = 384
    pieces = []
    for piece in (rows_send[..., :cut], rows_send[..., cut:]):
        piece_own = lax.all_to_all(piece, "chip", 0, 0, tiled=True)
        pieces.append(lax.all_gather(piece_own, "tp", axis=0, tiled=False))
    meta_all, pieces[1] = lax.optimization_barrier((meta_all, pieces[1]))
    rows_gathered = jnp.concatenate(pieces, axis=-1)
    rows_other = lax.ppermute(rows_gathered, "core", partner)
    all_rows = jnp.where(
        core == 0,
        jnp.concatenate([rows_gathered, rows_other], axis=1),
        jnp.concatenate([rows_other, rows_gathered], axis=1),
    )
    chip_range = jnp.arange(n_chips, dtype=jnp.int32)
    source_of = jnp.concatenate([2 * chip_range, 2 * chip_range + 1])
    all_meta = meta_all[source_of, chip]
    slab_rows = all_rows.shape[1] * all_rows.shape[2]
    rows_q = all_rows.reshape(n_tp, slab_rows, quarter_cols)
    rows_float = rows_q.astype(jnp.float32)
    row_scale = lax.rsqrt(
        jnp.mean(rows_float * rows_float, axis=(0, 2), keepdims=True) + norm_eps
    )
    gain_q = norm_gain.reshape(n_tp, 1, quarter_cols)
    normed = (rows_float * row_scale * gain_q).astype(jnp.bfloat16)
    gate_q = gate_up[0].reshape(n_tp, quarter_cols, 2, gate_up.shape[3])
    gate_and_up = jnp.einsum(
        "tnd,tdgf->ngf", normed, gate_q, preferred_element_type=jnp.float32
    )
    hidden = (jax.nn.silu(gate_and_up[:, 0, :]) * gate_and_up[:, 1, :]).astype(jnp.bfloat16)
    half_cols = quarter_cols // 2
    down_chunks = expert_down[0].reshape(expert_down.shape[1], n_tp, 2, half_cols)
    partial_out = jnp.einsum(
        "nf,fthd->htnd", hidden, down_chunks, preferred_element_type=jnp.float32
    ).astype(jnp.bfloat16)
    half_keep = lax.dynamic_index_in_dim(partial_out, core, 0, keepdims=False)
    half_send = lax.dynamic_index_in_dim(partial_out, 1 - core, 0, keepdims=False)
    half_recv = lax.ppermute(half_send, "core", partner)
    pair_sum = (half_keep.astype(jnp.float32) + half_recv.astype(jnp.float32)).astype(
        jnp.bfloat16
    )
    value_total = lax.psum_scatter(pair_sum, "tp", scatter_dimension=0, tiled=True)[0].astype(
        jnp.float32
    )
    own_rows = lax.dynamic_index_in_dim(rows_q, tp_index, 0, keepdims=False)
    own_half = lax.dynamic_index_in_dim(
        own_rows.reshape(slab_rows, 2, half_cols), core, 1, keepdims=False
    ).astype(jnp.float32)
    row_weight = all_meta[..., 1].astype(jnp.float32).reshape(slab_rows)
    result = (row_weight[:, None] * (value_total + own_half)).astype(jnp.bfloat16)
    result = result.reshape(all_meta.shape[0], all_meta.shape[1], half_cols)
    devices_req = 2 * n_chips
    device_range = jnp.arange(devices_req, dtype=jnp.int32)
    inverse = jnp.sum(
        device_range[:, None] * (batch_home[:, None] == device_range[None, :]).astype(jnp.int32),
        axis=0,
    )
    local_of = (inverse % 2) * n_chips + inverse // 2
    sent = result[local_of]
    returned = lax.all_to_all(sent, ("chip", "core"), 0, 0, tiled=True)
    home_batch = inverse[2 * chip + core]
    flat_rows = (
        returned.reshape(n_chips, 2, all_meta.shape[1], half_cols)
        .transpose(0, 2, 1, 3)
        .reshape(-1, quarter_cols)
    )
    flat_token = meta_all[home_batch, :, :, 0].reshape(-1).astype(jnp.int32)
    selector = (jnp.arange(tokens, dtype=jnp.int32)[:, None] == flat_token[None, :]).astype(
        jnp.bfloat16
    )
    return jnp.dot(selector, flat_rows, preferred_element_type=jnp.float32).astype(jnp.bfloat16)


def solution(mesh):
    req = ("chip", "core")
    n_req, n_tp = mesh.devices.shape
    split_mesh = Mesh(mesh.devices.reshape(n_req // 2, 2, n_tp), ("chip", "core", "tp"))
    placed = (
        P(req, "tp"),
        P(req, "tp"),
        P(req, None, "tp"),
        P(None, req, None, "tp"),
        P("tp"),
        P(req),
        P(req),
        P(),
        P(req, None),
        P(req, None),
        P(),
        P("tp", None),
        P(req, None, None, "tp"),
        P(req, "tp", None),
    )
    return jax.shard_map(
        body, mesh=split_mesh, in_specs=placed, out_specs=P(req, "tp"), check_vma=False
    )
```
